256 devices in a mesh: section: 8 (over z), ctx: 32 (over x, y, core).
Axes of the slice: x: 4, y: 4, z: 8, core: 2. Of those that a mesh axis runs over, the one named last changes fastest.
Arguments:
- query_rows: bfloat16 [8, 8192, 2048], P('section', 'ctx'), may hold values from -40 to 40
- key_rows: bfloat16 [8, 8192, 1024], P('section', 'ctx'), may hold values from -6 to 6
- value_rows: bfloat16 [8, 8192, 1024], P('section', 'ctx'), may hold values from -6 to 6
- finished_grad: bfloat16 [8, 8192, 2048], P('section', 'ctx'), may hold values from -96 to 96
- doc_lengths: int32 [4], replicated, may hold values from 1 to 4096, as said below
Outputs:
- query_grad: bfloat16 [8, 8192, 2048], P('section', 'ctx')
- key_grad: bfloat16 [8, 8192, 1024], P('section', 'ctx')
- value_grad: bfloat16 [8, 8192, 1024], P('section', 'ctx')
The draws below stay inside these ranges and needn't reach their ends.
Inputs may be any that keep to these rules, and one draw needn't show every extreme that they name: `doc_lengths`: document lengths add up to 8192; the longest is exactly 4096.
All inputs are finite; a program needn't handle non-finite values.
Results may differ from the reference program's by a relative error of at most 0.04.
Values may be sent and summed in bfloat16 or wider, within the bound.
No kernel may reach another device: no remote copies, remote signals or barrier semaphores. Data moves between devices by JAX's collectives and lax.ppermute only.
A program may use at most 128 MiB of HBM per device.

```python
import jax
import jax.numpy as jnp
from jax import lax

ROWS = 256
WINDOW = 1024
HEADS = 16
KV_HEADS = 8
HEAD_DIM = 128
GROUP = 2
SECTIONS = 8
SEQ = 8192
MOST_DOC = 4096


def draw_key_rows(key, part):
    drawn = jax.random.truncated_normal(jax.random.fold_in(key, 101), -6.0, 6.0, (SECTIONS, SEQ, KV_HEADS * HEAD_DIM), jnp.float32)
    return drawn.astype(jnp.bfloat16)


def draw_query_rows(key, part):
    drawn = jax.random.truncated_normal(jax.random.fold_in(key, 201), -6.0, 6.0, (SECTIONS, SEQ, HEADS * HEAD_DIM), jnp.float32)
    return drawn.astype(jnp.bfloat16)


def draw_doc_lengths(key, part):
    remain = SEQ - MOST_DOC
    first_most = max(1, remain - WINDOW)
    first_len = jax.random.randint(jax.random.fold_in(key, 301), (), 1, first_most + 1).astype(jnp.int32)
    rest = (remain - first_len).astype(jnp.int32)
    third_len = jax.random.randint(jax.random.fold_in(key, 302), (), 1, rest).astype(jnp.int32)
    fourth_len = (rest - third_len).astype(jnp.int32)
    return jnp.stack([first_len, jnp.int32(MOST_DOC), third_len, fourth_len]).astype(jnp.int32)


def block_levels(own_key, dims, pieces, low, largest):
    gain = 1.0
    for dim, parts in pieces:
        heights = jax.random.uniform(jax.random.fold_in(jax.random.fold_in(own_key, 6), dim), (parts,), jnp.float32, low / len(pieces), largest / len(pieces))
        gain = gain * jnp.repeat(jnp.exp(heights), dims[dim] // parts).reshape((-1,) + (1,) * (len(dims) - 1 - dim))
    return gain


def scatter_about(own_key, shape, deviation, reach, cuts=(), kind=jnp.bfloat16):
    factor_of = block_levels(own_key, shape, cuts, -0.22, 0.18) if cuts else 1.0
    result = jax.random.normal(own_key, shape, jnp.float32) * deviation * factor_of
    return jnp.minimum(jnp.maximum(result, -reach), reach).astype(kind)


def setup_inputs(seed: int = 0) -> dict:
    arg_keys = jax.random.split(jax.random.key(seed), 6)
    query_rows = draw_query_rows(jax.random.fold_in(arg_keys[5], 71), 0)
    key_rows = draw_key_rows(jax.random.fold_in(arg_keys[5], 71), 0)
    value_rows = scatter_about(arg_keys[2], (SECTIONS, SEQ, KV_HEADS * HEAD_DIM), 1.0, 6.0, ((0, 8), (1, 32)))
    finished_grad = scatter_about(arg_keys[3], (SECTIONS, SEQ, HEADS * HEAD_DIM), 16.0, 96.0, ((0, 8), (1, 32)))
    doc_lengths = draw_doc_lengths(jax.random.fold_in(arg_keys[5], 71), 0)
    return dict(query_rows=query_rows, key_rows=key_rows, value_rows=value_rows, finished_grad=finished_grad, doc_lengths=doc_lengths)


SCORE_SCALE = 168.0 ** -0.5


def doc_number(positions, doc_lengths):
    ends = jnp.cumsum(doc_lengths).astype(jnp.int32)
    return jnp.sum((positions[:, None] >= ends[None, :]).astype(jnp.int32), axis=1).astype(jnp.int32)


def window_mask(query_pos, key_pos, doc_lengths):
    same_doc = doc_number(query_pos, doc_lengths)[:, None] == doc_number(key_pos, doc_lengths)[None, :]
    spacing = query_pos[:, None] - key_pos[None, :]
    return same_doc & (spacing >= 0) & (spacing < WINDOW) & (key_pos[None, :] >= 0)


def to_half(values):
    return lax.optimization_barrier(values.astype(jnp.bfloat16)).astype(jnp.float32)


def split_round(block_term):
    return jnp.concatenate([to_half(block_term[:WINDOW]), block_term[WINDOW:]], axis=0)


def section_grads(queries, keys_in, values_in, arriving, doc_lengths):
    span = WINDOW + ROWS
    width = keys_in.shape[1]
    padded_keys = jnp.concatenate([jnp.zeros((WINDOW, width), keys_in.dtype), keys_in], axis=0)
    padded_values = jnp.concatenate([jnp.zeros((WINDOW, width), values_in.dtype), values_in], axis=0)

    def step(carry, block):
        acc_keys, acc_values = carry
        start = (block * ROWS).astype(jnp.int32)
        query_block = lax.dynamic_slice_in_dim(queries, start, ROWS, 0).astype(jnp.float32).reshape(ROWS, KV_HEADS, GROUP, HEAD_DIM)
        grad_block = lax.dynamic_slice_in_dim(arriving, start, ROWS, 0).astype(jnp.float32).reshape(ROWS, KV_HEADS, GROUP, HEAD_DIM)
        key_block = lax.dynamic_slice_in_dim(padded_keys, start, span, 0).astype(jnp.float32).reshape(span, KV_HEADS, HEAD_DIM)
        value_block = lax.dynamic_slice_in_dim(padded_values, start, span, 0).astype(jnp.float32).reshape(span, KV_HEADS, HEAD_DIM)
        query_pos = start + jnp.arange(ROWS, dtype=jnp.int32)
        key_pos = start - WINDOW + jnp.arange(span, dtype=jnp.int32)
        allowed = window_mask(query_pos, key_pos, doc_lengths)
        scores = SCORE_SCALE * jnp.einsum('rhjd,khd->hjrk', query_block, key_block)
        scores = jnp.where(allowed[None, None], scores, -jnp.inf)
        highest = jnp.max(scores, axis=-1, keepdims=True)
        log_total = highest + jnp.log(jnp.sum(jnp.exp(scores - highest), axis=-1, keepdims=True))
        weights = jnp.exp(scores - log_total)
        weight_half = to_half(weights)
        attended = to_half(jnp.einsum('hjrk,khd->rhjd', weight_half, value_block))
        row_dot = jnp.einsum('rhjd,rhjd->hjr', attended, grad_block)
        weight_grad = jnp.einsum('rhjd,khd->hjrk', grad_block, value_block)
        score_grad = to_half(weights * (weight_grad - row_dot[..., None]))
        grad_query = SCORE_SCALE * jnp.einsum('hjrk,khd->rhjd', score_grad, key_block)
        grad_keys = split_round((SCORE_SCALE * jnp.einsum('hjrk,rhjd->khd', score_grad, query_block)).reshape(span, width))
        grad_values = split_round(jnp.einsum('hjrk,rhjd->khd', weight_half, grad_block).reshape(span, width))
        acc_keys = lax.dynamic_update_slice_in_dim(acc_keys, lax.dynamic_slice_in_dim(acc_keys, start, span, 0) + grad_keys, start, 0)
        acc_values = lax.dynamic_update_slice_in_dim(acc_values, lax.dynamic_slice_in_dim(acc_values, start, span, 0) + grad_values, start, 0)
        return (acc_keys, acc_values), grad_query.reshape(ROWS, HEADS * HEAD_DIM).astype(jnp.bfloat16)

    empty = jnp.zeros((WINDOW + SEQ, width), jnp.float32)
    (acc_keys, acc_values), query_blocks = lax.scan(step, (empty, empty), jnp.arange(SEQ // ROWS, dtype=jnp.int32))
    return (query_blocks.reshape(SEQ, HEADS * HEAD_DIM), acc_keys[WINDOW:].astype(jnp.bfloat16), acc_values[WINDOW:].astype(jnp.bfloat16))


def reference(query_rows, key_rows, value_rows, finished_grad, doc_lengths):
    arriving = jnp.roll(finished_grad, -1, axis=0)

    def one_section(items):
        return section_grads(items[0], items[1], items[2], items[3], doc_lengths)

    query_grad, key_grad, value_grad = lax.map(one_section, (query_rows, key_rows, value_rows, arriving))
    return (query_grad, key_grad, value_grad)
```

```python
import jax
import jax.numpy as jnp
from jax import lax
from jax.sharding import PartitionSpec as P

WINDOW = 1024
KV_HEADS = 8


SCORE_SCALE = 168.0 ** (-0.5)


def passed_along(shard, axis, by):
    count = lax.axis_size(axis)
    return lax.ppermute(shard, axis, [(i, (i + by) % count) for i in range(count)])


def shifted(value, axis, steps):
    count = lax.axis_size(axis)
    initial, last = (max(0, -steps), min(count, count - steps))
    return lax.ppermute(value, axis, [(source, source + steps) for source in range(initial, last)])


def doc_number(positions, doc_lengths):
    ends = jnp.cumsum(doc_lengths)
    return jnp.sum((positions[:, None] >= ends[None, :]).astype(jnp.int32), axis=1)


def window_mask(query_pos, key_pos, doc_lengths):
    same_doc = (
        doc_number(query_pos, doc_lengths)[:, None] == doc_number(key_pos, doc_lengths)[None, :]
    )
    spacing = query_pos[:, None] - key_pos[None, :]
    return same_doc & (spacing >= 0) & (spacing < WINDOW) & (key_pos[None, :] >= 0)


def group_pass(query_part, key_part, value_part, grad_part, allowed):
    count_rows = query_part.shape[0]
    head_size = key_part.shape[1]
    query_head = query_part.reshape(count_rows, -1, head_size)
    grad_head = grad_part.reshape(count_rows, -1, head_size)
    scores = SCORE_SCALE * jnp.einsum(
        "rjd,kd->jrk", query_head, key_part, preferred_element_type=jnp.float32
    )
    scores = jnp.where(allowed[None], scores, -jnp.inf)
    highest = jnp.max(scores, axis=-1, keepdims=True)
    log_total = highest + jnp.log(jnp.sum(jnp.exp(scores - highest), axis=-1, keepdims=True))
    weights = jnp.exp(scores - log_total)
    weight_half = weights.astype(jnp.bfloat16)
    attended = jnp.einsum(
        "jrk,kd->rjd", weight_half, value_part, preferred_element_type=jnp.float32
    ).astype(jnp.bfloat16)
    row_dot = jnp.transpose(
        jnp.sum(attended.astype(jnp.float32) * grad_head.astype(jnp.float32), axis=-1)
    )
    weight_grad = jnp.einsum(
        "rjd,kd->jrk", grad_head, value_part, preferred_element_type=jnp.float32
    )
    score_grad = (weights * (weight_grad - row_dot[:, :, None])).astype(jnp.bfloat16)
    query_back = SCORE_SCALE * jnp.einsum(
        "jrk,kd->rjd", score_grad, key_part, preferred_element_type=jnp.float32
    )
    key_back = SCORE_SCALE * jnp.einsum(
        "jrk,rjd->kd", score_grad, query_head, preferred_element_type=jnp.float32
    )
    value_back = jnp.einsum(
        "jrk,rjd->kd", weight_half, grad_head, preferred_element_type=jnp.float32
    )
    return (query_back.reshape(count_rows, -1), key_back, value_back, log_total[:, :, 0], row_dot)


def local(query_rows, key_rows, value_rows, finished_grad, doc_lengths):
    queries = query_rows[0]
    keys_here = key_rows[0]
    values_here = value_rows[0]
    count_rows = queries.shape[0]
    reach_blocks = WINDOW // count_rows
    pair_width = keys_here.shape[1]
    head_size = pair_width // KV_HEADS
    group_width = queries.shape[1] // KV_HEADS
    heads_group = group_width // head_size
    rank_here = lax.axis_index("ctx")
    first_pos = rank_here * count_rows
    arriving = passed_along(finished_grad, "section", -1)[0]
    own_pair = jnp.stack([keys_here, values_here])
    pieces = [own_pair]
    relayed = own_pair
    for _ in range(reach_blocks):
        relayed = shifted(relayed, "ctx", 1)
        pieces.insert(0, relayed)
    window_pair = jnp.concatenate(pieces, axis=1)
    span = window_pair.shape[1]
    query_pos = first_pos + jnp.arange(count_rows, dtype=jnp.int32)
    key_pos = first_pos - WINDOW + jnp.arange(span, dtype=jnp.int32)
    allowed = window_mask(query_pos, key_pos, doc_lengths)

    def per_group(group, carry):
        query_acc, keys_acc, values_acc, log_totals, row_dots = carry
        query_part = lax.dynamic_slice_in_dim(queries, group * group_width, group_width, 1)
        grad_part = lax.dynamic_slice_in_dim(arriving, group * group_width, group_width, 1)
        key_part = lax.dynamic_slice_in_dim(window_pair[0], group * head_size, head_size, 1)
        value_part = lax.dynamic_slice_in_dim(window_pair[1], group * head_size, head_size, 1)
        query_back, key_back, value_back, log_total, row_dot = group_pass(
            query_part, key_part, value_part, grad_part, allowed
        )
        query_acc = lax.dynamic_update_slice_in_dim(
            query_acc, query_back.astype(jnp.bfloat16), group * group_width, 1
        )
        keys_acc = lax.dynamic_update_slice_in_dim(keys_acc, key_back, group * head_size, 1)
        values_acc = lax.dynamic_update_slice_in_dim(values_acc, value_back, group * head_size, 1)
        log_totals = lax.dynamic_update_slice_in_dim(log_totals, log_total, group * heads_group, 0)
        row_dots = lax.dynamic_update_slice_in_dim(row_dots, row_dot, group * heads_group, 0)
        return (query_acc, keys_acc, values_acc, log_totals, row_dots)

    start_carry = (
        jnp.zeros(queries.shape, jnp.bfloat16),
        jnp.zeros((span, pair_width), jnp.float32),
        jnp.zeros((span, pair_width), jnp.float32),
        jnp.zeros((KV_HEADS * heads_group, count_rows), jnp.float32),
        jnp.zeros((KV_HEADS * heads_group, count_rows), jnp.float32),
    )
    grad_query, grad_keys, grad_values, log_totals, row_dots = lax.fori_loop(
        0, KV_HEADS, per_group, start_carry
    )
    own_start = reach_blocks * count_rows
    grad_pair = jnp.stack([grad_keys, grad_values])
    partial = grad_pair[:, :count_rows].astype(jnp.bfloat16)
    for block in range(1, reach_blocks):
        term = grad_pair[:, block * count_rows : (block + 1) * count_rows]
        arrived = shifted(partial, "ctx", -1).astype(jnp.float32)
        partial = (arrived + term.astype(jnp.bfloat16).astype(jnp.float32)).astype(jnp.bfloat16)
    key_total = grad_pair[:, own_start:] + shifted(partial, "ctx", -1).astype(jnp.float32)
    return (
        grad_query[None],
        key_total[0].astype(jnp.bfloat16)[None],
        key_total[1].astype(jnp.bfloat16)[None],
    )


def solution(mesh):
    return jax.shard_map(
        local,
        mesh=mesh,
        in_specs=(
            P("section", "ctx", None),
            P("section", "ctx", None),
            P("section", "ctx", None),
            P("section", "ctx", None),
            P(),
        ),
        out_specs=(P("section", "ctx", None), P("section", "ctx", None), P("section", "ctx", None)),
        check_vma=False,
    )
```

```python
import jax
import jax.numpy as jnp
from jax import lax
from jax.experimental import pallas as pl
from jax.experimental.pallas import tpu as pltpu
from jax.sharding import PartitionSpec as P

WINDOW = 1024
KV_HEADS = 8


SCORE_SCALE = 168.0 ** (-0.5)


def product(a, b, dims):
    return lax.dot_general(a, b, dims, preferred_element_type=jnp.float32)


def attention_back_kernel(q_ref, do_ref, k_ref, v_ref, mask_ref, dq_ref, dk_ref, dv_ref):
    head_size = k_ref.shape[1]
    heads = q_ref.shape[1] // head_size
    allowed = mask_ref[...] > 0
    keys = k_ref[...]
    values = v_ref[...]
    queries = jnp.concatenate([q_ref[:, h * head_size:(h + 1) * head_size] for h in range(heads)], axis=0)
    grads = jnp.concatenate([do_ref[:, h * head_size:(h + 1) * head_size] for h in range(heads)], axis=0)
    allowed = jnp.concatenate([allowed] * heads, axis=0)
    nt = (((1,), (1,)), ((), ()))
    tn = (((0,), (0,)), ((), ()))
    nn = (((1,), (0,)), ((), ()))
    scores = SCORE_SCALE * product(queries, keys, nt)
    scores = jnp.where(allowed, scores, -jnp.inf)
    highest = jnp.max(scores, axis=-1, keepdims=True)
    log_total = highest + jnp.log(jnp.sum(jnp.exp(scores - highest), axis=-1, keepdims=True))
    weights = jnp.exp(scores - log_total)
    weight_half = weights.astype(jnp.bfloat16)
    attended = product(weight_half, values, nn).astype(jnp.bfloat16)
    row_dot = jnp.sum(attended.astype(jnp.float32) * grads.astype(jnp.float32), axis=-1, keepdims=True)
    weight_grad = product(grads, values, nt)
    score_grad = (weights * (weight_grad - row_dot)).astype(jnp.bfloat16)
    query_back = SCORE_SCALE * product(score_grad, keys, nn)
    rows = q_ref.shape[0]
    for h in range(heads):
        dq_ref[:, h * head_size:(h + 1) * head_size] = query_back[h * rows:(h + 1) * rows].astype(dq_ref.dtype)
    dk_ref[...] = SCORE_SCALE * product(score_grad, queries, tn)
    dv_ref[...] = product(weight_half, grads, tn)


def attention_back(queries, grads, window_keys, window_values, allowed, groups):
    rows, width = queries.shape
    span, pair_width = window_keys.shape
    head_size = pair_width // groups
    group_width = width // groups
    q_spec = pl.BlockSpec((rows, group_width), lambda g: (0, g))
    kv_spec = pl.BlockSpec((span, head_size), lambda g: (0, g))
    mask_spec = pl.BlockSpec((rows, span), lambda g: (0, 0))
    return pl.pallas_call(
        attention_back_kernel,
        grid=(groups,),
        in_specs=[q_spec, q_spec, kv_spec, kv_spec, mask_spec],
        out_specs=[q_spec, kv_spec, kv_spec],
        out_shape=[
            jax.ShapeDtypeStruct((rows, width), jnp.bfloat16),
            jax.ShapeDtypeStruct((span, pair_width), jnp.float32),
            jax.ShapeDtypeStruct((span, pair_width), jnp.float32),
        ],
        compiler_params=pltpu.CompilerParams(vmem_limit_bytes=60 * 1024 * 1024),
    )(queries, grads, window_keys, window_values, allowed)


def passed_along(shard, axis, by):
    count = lax.axis_size(axis)
    return lax.ppermute(shard, axis, [(i, (i + by) % count) for i in range(count)])


def shifted(value, axis, steps):
    count = lax.axis_size(axis)
    initial, last = (max(0, -steps), min(count, count - steps))
    return lax.ppermute(value, axis, [(source, source + steps) for source in range(initial, last)])


def doc_number(positions, doc_lengths):
    ends = jnp.cumsum(doc_lengths)
    return jnp.sum((positions[:, None] >= ends[None, :]).astype(jnp.int32), axis=1)


def window_mask(query_pos, key_pos, doc_lengths):
    same_doc = (
        doc_number(query_pos, doc_lengths)[:, None] == doc_number(key_pos, doc_lengths)[None, :]
    )
    spacing = query_pos[:, None] - key_pos[None, :]
    return same_doc & (spacing >= 0) & (spacing < WINDOW) & (key_pos[None, :] >= 0)


def group_pass(query_part, key_part, value_part, grad_part, allowed):
    count_rows = query_part.shape[0]
    head_size = key_part.shape[1]
    query_head = query_part.reshape(count_rows, -1, head_size)
    grad_head = grad_part.reshape(count_rows, -1, head_size)
    scores = SCORE_SCALE * jnp.einsum(
        "rjd,kd->jrk", query_head, key_part, preferred_element_type=jnp.float32
    )
    scores = jnp.where(allowed[None], scores, -jnp.inf)
    highest = jnp.max(scores, axis=-1, keepdims=True)
    log_total = highest + jnp.log(jnp.sum(jnp.exp(scores - highest), axis=-1, keepdims=True))
    weights = jnp.exp(scores - log_total)
    weight_half = weights.astype(jnp.bfloat16)
    attended = jnp.einsum(
        "jrk,kd->rjd", weight_half, value_part, preferred_element_type=jnp.float32
    ).astype(jnp.bfloat16)
    row_dot = jnp.transpose(
        jnp.sum(attended.astype(jnp.float32) * grad_head.astype(jnp.float32), axis=-1)
    )
    weight_grad = jnp.einsum(
        "rjd,kd->jrk", grad_head, value_part, preferred_element_type=jnp.float32
    )
    score_grad = (weights * (weight_grad - row_dot[:, :, None])).astype(jnp.bfloat16)
    query_back = SCORE_SCALE * jnp.einsum(
        "jrk,kd->rjd", score_grad, key_part, preferred_element_type=jnp.float32
    )
    key_back = SCORE_SCALE * jnp.einsum(
        "jrk,rjd->kd", score_grad, query_head, preferred_element_type=jnp.float32
    )
    value_back = jnp.einsum(
        "jrk,rjd->kd", weight_half, grad_head, preferred_element_type=jnp.float32
    )
    return (query_back.reshape(count_rows, -1), key_back, value_back, log_total[:, :, 0], row_dot)


def local(query_rows, key_rows, value_rows, finished_grad, doc_lengths):
    queries = query_rows[0]
    keys_here = key_rows[0]
    values_here = value_rows[0]
    count_rows = queries.shape[0]
    reach_blocks = WINDOW // count_rows
    pair_width = keys_here.shape[1]
    head_size = pair_width // KV_HEADS
    group_width = queries.shape[1] // KV_HEADS
    heads_group = group_width // head_size
    rank_here = lax.axis_index("ctx")
    first_pos = rank_here * count_rows
    arriving = passed_along(finished_grad, "section", -1)[0]
    own_pair = jnp.stack([keys_here, values_here])
    pieces = [own_pair]
    relayed = own_pair
    for _ in range(reach_blocks):
        relayed = shifted(relayed, "ctx", 1)
        pieces.insert(0, relayed)
    window_pair = jnp.concatenate(pieces, axis=1)
    span = window_pair.shape[1]
    query_pos = first_pos + jnp.arange(count_rows, dtype=jnp.int32)
    key_pos = first_pos - WINDOW + jnp.arange(span, dtype=jnp.int32)
    allowed = window_mask(query_pos, key_pos, doc_lengths)

    grad_query, grad_keys, grad_values = attention_back(
        queries, arriving, window_pair[0], window_pair[1], allowed.astype(jnp.float32), KV_HEADS
    )
    own_start = reach_blocks * count_rows
    grad_pair = jnp.stack([grad_keys, grad_values])
    partial = grad_pair[:, :count_rows].astype(jnp.bfloat16)
    for block in range(1, reach_blocks):
        term = grad_pair[:, block * count_rows : (block + 1) * count_rows]
        arrived = shifted(partial, "ctx", -1).astype(jnp.float32)
        partial = (arrived + term.astype(jnp.bfloat16).astype(jnp.float32)).astype(jnp.bfloat16)
    key_total = grad_pair[:, own_start:] + shifted(partial, "ctx", -1).astype(jnp.float32)
    return (
        grad_query[None],
        key_total[0].astype(jnp.bfloat16)[None],
        key_total[1].astype(jnp.bfloat16)[None],
    )


def solution(mesh):
    return jax.shard_map(
        local,
        mesh=mesh,
        in_specs=(
            P("section", "ctx", None),
            P("section", "ctx", None),
            P("section", "ctx", None),
            P("section", "ctx", None),
            P(),
        ),
        out_specs=(P("section", "ctx", None), P("section", "ctx", None), P("section", "ctx", None)),
        check_vma=False,
    )
```

```python
import jax
import jax.numpy as jnp
from jax import lax
from jax.experimental import pallas as pl
from jax.experimental.pallas import tpu as pltpu
from jax.sharding import PartitionSpec as P

WINDOW = 1024
KV_HEADS = 8
CHUNKS = 2


SCORE_SCALE = 168.0 ** (-0.5)


def product(a, b, dims):
    return lax.dot_general(a, b, dims, preferred_element_type=jnp.float32)


def attention_back_kernel(
    q_ref, do_ref, k_ref, v_ref, mask_ref, dq_ref, dk_far_ref, dv_far_ref, dk_own_ref, dv_own_ref
):
    head_size = k_ref.shape[1]
    heads = q_ref.shape[1] // head_size
    rows = q_ref.shape[0]
    far = dk_far_ref.shape[0]
    allowed = mask_ref[...] > 0
    keys = k_ref[...]
    values = v_ref[...]
    queries = jnp.concatenate([q_ref[:, h * head_size:(h + 1) * head_size] for h in range(heads)], axis=0)
    grads = jnp.concatenate([do_ref[:, h * head_size:(h + 1) * head_size] for h in range(heads)], axis=0)
    allowed = jnp.concatenate([allowed] * heads, axis=0)
    nt = (((1,), (1,)), ((), ()))
    tn = (((0,), (0,)), ((), ()))
    nn = (((1,), (0,)), ((), ()))
    scores = SCORE_SCALE * product(queries, keys, nt)
    scores = jnp.where(allowed, scores, -jnp.inf)
    highest = jnp.max(scores, axis=-1, keepdims=True)
    log_total = highest + jnp.log(jnp.sum(jnp.exp(scores - highest), axis=-1, keepdims=True))
    weights = jnp.exp(scores - log_total)
    weight_half = weights.astype(jnp.bfloat16)
    attended = product(weight_half, values, nn).astype(jnp.bfloat16)
    row_dot = jnp.sum(attended.astype(jnp.float32) * grads.astype(jnp.float32), axis=-1, keepdims=True)
    weight_grad = product(grads, values, nt)
    score_grad = (weights * (weight_grad - row_dot)).astype(jnp.bfloat16)
    query_back = SCORE_SCALE * product(score_grad, keys, nn)
    for h in range(heads):
        dq_ref[:, h * head_size:(h + 1) * head_size] = query_back[h * rows:(h + 1) * rows].astype(dq_ref.dtype)
    key_back = SCORE_SCALE * product(score_grad, queries, tn)
    value_back = product(weight_half, grads, tn)
    dk_far_ref[...] = key_back[:far].astype(dk_far_ref.dtype)
    dv_far_ref[...] = value_back[:far].astype(dv_far_ref.dtype)
    dk_own_ref[...] = key_back[far:]
    dv_own_ref[...] = value_back[far:]


def attention_back(queries, grads, window_keys, window_values, allowed, first_group, groups):
    rows, width = queries.shape
    span, pair_width = window_keys.shape
    head_size = pair_width // groups
    group_width = 2 * head_size
    far = span - rows
    q_spec = pl.BlockSpec((rows, group_width), lambda g: (0, g + first_group))
    dq_spec = pl.BlockSpec((rows, group_width), lambda g: (0, g))
    kv_spec = pl.BlockSpec((span, head_size), lambda g: (0, g))
    far_spec = pl.BlockSpec((far, head_size), lambda g: (0, g))
    own_spec = pl.BlockSpec((rows, head_size), lambda g: (0, g))
    mask_spec = pl.BlockSpec((rows, span), lambda g: (0, 0))
    return pl.pallas_call(
        attention_back_kernel,
        grid=(groups,),
        in_specs=[q_spec, q_spec, kv_spec, kv_spec, mask_spec],
        out_specs=[dq_spec, far_spec, far_spec, own_spec, own_spec],
        out_shape=[
            jax.ShapeDtypeStruct((rows, groups * group_width), jnp.bfloat16),
            jax.ShapeDtypeStruct((far, pair_width), jnp.bfloat16),
            jax.ShapeDtypeStruct((far, pair_width), jnp.bfloat16),
            jax.ShapeDtypeStruct((rows, pair_width), jnp.float32),
            jax.ShapeDtypeStruct((rows, pair_width), jnp.float32),
        ],
        compiler_params=pltpu.CompilerParams(vmem_limit_bytes=60 * 1024 * 1024),
    )(queries, grads, window_keys, window_values, allowed)


def passed_along(shard, axis, by):
    count = lax.axis_size(axis)
    return lax.ppermute(shard, axis, [(i, (i + by) % count) for i in range(count)])


def shifted(value, axis, steps):
    count = lax.axis_size(axis)
    initial, last = (max(0, -steps), min(count, count - steps))
    return lax.ppermute(value, axis, [(source, source + steps) for source in range(initial, last)])


def doc_number(positions, doc_lengths):
    ends = jnp.cumsum(doc_lengths)
    return jnp.sum((positions[:, None] >= ends[None, :]).astype(jnp.int32), axis=1)


def window_mask(query_pos, key_pos, doc_lengths):
    same_doc = (
        doc_number(query_pos, doc_lengths)[:, None] == doc_number(key_pos, doc_lengths)[None, :]
    )
    spacing = query_pos[:, None] - key_pos[None, :]
    return same_doc & (spacing >= 0) & (spacing < WINDOW) & (key_pos[None, :] >= 0)


def group_pass(query_part, key_part, value_part, grad_part, allowed):
    count_rows = query_part.shape[0]
    head_size = key_part.shape[1]
    query_head = query_part.reshape(count_rows, -1, head_size)
    grad_head = grad_part.reshape(count_rows, -1, head_size)
    scores = SCORE_SCALE * jnp.einsum(
        "rjd,kd->jrk", query_head, key_part, preferred_element_type=jnp.float32
    )
    scores = jnp.where(allowed[None], scores, -jnp.inf)
    highest = jnp.max(scores, axis=-1, keepdims=True)
    log_total = highest + jnp.log(jnp.sum(jnp.exp(scores - highest), axis=-1, keepdims=True))
    weights = jnp.exp(scores - log_total)
    weight_half = weights.astype(jnp.bfloat16)
    attended = jnp.einsum(
        "jrk,kd->rjd", weight_half, value_part, preferred_element_type=jnp.float32
    ).astype(jnp.bfloat16)
    row_dot = jnp.transpose(
        jnp.sum(attended.astype(jnp.float32) * grad_head.astype(jnp.float32), axis=-1)
    )
    weight_grad = jnp.einsum(
        "rjd,kd->jrk", grad_head, value_part, preferred_element_type=jnp.float32
    )
    score_grad = (weights * (weight_grad - row_dot[:, :, None])).astype(jnp.bfloat16)
    query_back = SCORE_SCALE * jnp.einsum(
        "jrk,kd->rjd", score_grad, key_part, preferred_element_type=jnp.float32
    )
    key_back = SCORE_SCALE * jnp.einsum(
        "jrk,rjd->kd", score_grad, query_head, preferred_element_type=jnp.float32
    )
    value_back = jnp.einsum(
        "jrk,rjd->kd", weight_half, grad_head, preferred_element_type=jnp.float32
    )
    return (query_back.reshape(count_rows, -1), key_back, value_back, log_total[:, :, 0], row_dot)


def local(query_rows, key_rows, value_rows, finished_grad, doc_lengths):
    queries = query_rows[0]
    keys_here = key_rows[0]
    values_here = value_rows[0]
    count_rows = queries.shape[0]
    reach_blocks = WINDOW // count_rows
    pair_width = keys_here.shape[1]
    head_size = pair_width // KV_HEADS
    group_width = queries.shape[1] // KV_HEADS
    heads_group = group_width // head_size
    rank_here = lax.axis_index("ctx")
    first_pos = rank_here * count_rows
    arriving = passed_along(finished_grad, "section", -1)[0]
    query_pos = first_pos + jnp.arange(count_rows, dtype=jnp.int32)
    key_pos = first_pos - WINDOW + jnp.arange(WINDOW + count_rows, dtype=jnp.int32)
    allowed = window_mask(query_pos, key_pos, doc_lengths).astype(jnp.float32)
    chunk_groups = KV_HEADS // CHUNKS
    chunk_width = chunk_groups * head_size
    query_grads, key_grads, value_grads = [], [], []
    for chunk in range(CHUNKS):
        cols = slice(chunk * chunk_width, (chunk + 1) * chunk_width)
        own_pair = jnp.stack([keys_here[:, cols], values_here[:, cols]])
        pieces = [own_pair]
        relayed = own_pair
        for _ in range(reach_blocks):
            relayed = shifted(relayed, "ctx", 1)
            pieces.insert(0, relayed)
        window_pair = jnp.concatenate(pieces, axis=1)
        grad_query, keys_far, values_far, keys_own, values_own = attention_back(
            queries, arriving, window_pair[0], window_pair[1], allowed, chunk * chunk_groups, chunk_groups
        )
        far_pair = jnp.stack([keys_far, values_far])
        partial = far_pair[:, :count_rows]
        for block in range(1, reach_blocks):
            term = far_pair[:, block * count_rows : (block + 1) * count_rows].astype(jnp.float32)
            arrived = shifted(partial, "ctx", -1).astype(jnp.float32)
            partial = (arrived + term).astype(jnp.bfloat16)
        arrived = shifted(partial, "ctx", -1).astype(jnp.float32)
        query_grads.append(grad_query)
        key_grads.append((keys_own + arrived[0]).astype(jnp.bfloat16))
        value_grads.append((values_own + arrived[1]).astype(jnp.bfloat16))
    return (
        jnp.concatenate(query_grads, axis=1)[None],
        jnp.concatenate(key_grads, axis=1)[None],
        jnp.concatenate(value_grads, axis=1)[None],
    )


def solution(mesh):
    return jax.shard_map(
        local,
        mesh=mesh,
        in_specs=(
            P("section", "ctx", None),
            P("section", "ctx", None),
            P("section", "ctx", None),
            P("section", "ctx", None),
            P(),
        ),
        out_specs=(P("section", "ctx", None), P("section", "ctx", None), P("section", "ctx", None)),
        check_vma=False,
    )
```

```python
import jax
import jax.numpy as jnp
from jax import lax
from jax.experimental import pallas as pl
from jax.experimental.pallas import tpu as pltpu
from jax.sharding import PartitionSpec as P


WINDOW = 1024
KV_HEADS = 8
CHUNKS = 2
GROUP = 2


SCORE_SCALE = 168.0 ** (-0.5)


def product(a, b, dims):
    return lax.dot_general(a, b, dims, preferred_element_type=jnp.float32)


def attention_back_kernel(
    at_ref, q_ref, do_ref, k_ref, v_ref, mask_ref, dq_ref, dk_far_ref, dv_far_ref, dk_own_ref, dv_own_ref
):
    head_size = k_ref.shape[1]
    heads = q_ref.shape[1] // head_size
    rows = q_ref.shape[0]
    far = dk_far_ref.shape[0]
    allowed = mask_ref[...] > 0
    keys = k_ref[...]
    values = v_ref[...]
    queries = jnp.concatenate([q_ref[:, h * head_size:(h + 1) * head_size] for h in range(heads)], axis=0)
    grads = jnp.concatenate([do_ref[:, h * head_size:(h + 1) * head_size] for h in range(heads)], axis=0)
    allowed = jnp.concatenate([allowed] * heads, axis=0)
    nt = (((1,), (1,)), ((), ()))
    tn = (((0,), (0,)), ((), ()))
    nn = (((1,), (0,)), ((), ()))
    scores = SCORE_SCALE * product(queries, keys, nt)
    scores = jnp.where(allowed, scores, -jnp.inf)
    highest = jnp.max(scores, axis=-1, keepdims=True)
    log_total = highest + jnp.log(jnp.sum(jnp.exp(scores - highest), axis=-1, keepdims=True))
    weights = jnp.exp(scores - log_total)
    weight_half = weights.astype(jnp.bfloat16)
    attended = product(weight_half, values, nn).astype(jnp.bfloat16)
    row_dot = jnp.sum(attended.astype(jnp.float32) * grads.astype(jnp.float32), axis=-1, keepdims=True)
    weight_grad = product(grads, values, nt)
    score_grad = (weights * (weight_grad - row_dot)).astype(jnp.bfloat16)
    query_back = SCORE_SCALE * product(score_grad, keys, nn)
    for h in range(heads):
        dq_ref[:, h * head_size:(h + 1) * head_size] = query_back[h * rows:(h + 1) * rows].astype(dq_ref.dtype)
    key_back = SCORE_SCALE * product(score_grad, queries, tn)
    value_back = product(weight_half, grads, tn)
    dk_far_ref[...] = key_back[:far].astype(dk_far_ref.dtype)
    dv_far_ref[...] = value_back[:far].astype(dv_far_ref.dtype)
    dk_own_ref[...] = key_back[far:]
    dv_own_ref[...] = value_back[far:]


def attention_back(queries, grads, window_keys, window_values, allowed, first_group, kv_group, groups):
    rows, width = queries.shape
    span = window_keys.shape[0]
    head_size = width // (GROUP * KV_HEADS)
    pair_width = groups * head_size
    group_width = GROUP * head_size
    far = span - rows
    q_spec = pl.BlockSpec((rows, group_width), lambda g, at: (0, g + at[0]))
    dq_spec = pl.BlockSpec((rows, group_width), lambda g, at: (0, g))
    kv_spec = pl.BlockSpec((span, head_size), lambda g, at: (0, g + at[1]))
    far_spec = pl.BlockSpec((far, head_size), lambda g, at: (0, g))
    own_spec = pl.BlockSpec((rows, head_size), lambda g, at: (0, g))
    mask_spec = pl.BlockSpec((rows, span), lambda g, at: (0, 0))
    grid_spec = pltpu.PrefetchScalarGridSpec(
        num_scalar_prefetch=1,
        grid=(groups,),
        in_specs=[q_spec, q_spec, kv_spec, kv_spec, mask_spec],
        out_specs=[dq_spec, far_spec, far_spec, own_spec, own_spec],
    )
    return pl.pallas_call(
        attention_back_kernel,
        grid_spec=grid_spec,
        out_shape=[
            jax.ShapeDtypeStruct((rows, groups * group_width), jnp.bfloat16),
            jax.ShapeDtypeStruct((far, pair_width), jnp.bfloat16),
            jax.ShapeDtypeStruct((far, pair_width), jnp.bfloat16),
            jax.ShapeDtypeStruct((rows, pair_width), jnp.float32),
            jax.ShapeDtypeStruct((rows, pair_width), jnp.float32),
        ],
        compiler_params=pltpu.CompilerParams(vmem_limit_bytes=60 * 1024 * 1024),
    )(jnp.array([first_group, kv_group], jnp.int32), queries, grads, window_keys, window_values, allowed)


def passed_along(shard, axis, by):
    count = lax.axis_size(axis)
    return lax.ppermute(shard, axis, [(i, (i + by) % count) for i in range(count)])


def shifted(value, axis, steps):
    count = lax.axis_size(axis)
    initial, last = (max(0, -steps), min(count, count - steps))
    return lax.ppermute(value, axis, [(source, source + steps) for source in range(initial, last)])


def doc_number(positions, doc_lengths):
    ends = jnp.cumsum(doc_lengths)
    return jnp.sum((positions[:, None] >= ends[None, :]).astype(jnp.int32), axis=1)


def window_mask(query_pos, key_pos, doc_lengths):
    same_doc = (
        doc_number(query_pos, doc_lengths)[:, None] == doc_number(key_pos, doc_lengths)[None, :]
    )
    spacing = query_pos[:, None] - key_pos[None, :]
    return same_doc & (spacing >= 0) & (spacing < WINDOW) & (key_pos[None, :] >= 0)


def local_body(query_rows, key_rows, value_rows, finished_grad, doc_lengths):
    queries = query_rows[0]
    keys_here = key_rows[0]
    values_here = value_rows[0]
    count_rows = queries.shape[0]
    reach_blocks = WINDOW // count_rows
    pair_width = keys_here.shape[1]
    head_size = pair_width // KV_HEADS
    rank_here = lax.axis_index("ctx")
    first_pos = rank_here * count_rows
    arriving = passed_along(finished_grad, "section", -1)[0]
    query_pos = first_pos + jnp.arange(count_rows, dtype=jnp.int32)
    key_pos = first_pos - WINDOW + jnp.arange(WINDOW + count_rows, dtype=jnp.int32)
    allowed = window_mask(query_pos, key_pos, doc_lengths).astype(jnp.float32)
    chunk_groups = KV_HEADS // CHUNKS
    chunk_width = chunk_groups * head_size

    def own_pair_of(chunk):
        cols = slice(chunk * chunk_width, (chunk + 1) * chunk_width)
        return jnp.stack([keys_here[:, cols], values_here[:, cols]])

    def joined(*values):
        return lax.optimization_barrier(values)

    def far_payload(pieces, block):
        rows = slice(block * count_rows, (block + 1) * count_rows)
        return jnp.stack(
            [
                jnp.concatenate([piece[1][rows] for piece in pieces], axis=1),
                jnp.concatenate([piece[2][rows] for piece in pieces], axis=1),
            ]
        )

    def return_hop(partial, pieces, block):
        arrived = shifted(partial, "ctx", -1).astype(jnp.float32)
        return (arrived + far_payload(pieces, block).astype(jnp.float32)).astype(jnp.bfloat16)

    def run_chunk(chunk, window_pair, side_step, side_value):
        pieces = []
        tied = (queries, arriving, window_pair)
        for group in range(chunk_groups):
            side_value = side_step(group, side_value)
            piece = attention_back(
                tied[0], tied[1], tied[2][0], tied[2][1], allowed,
                chunk * chunk_groups + group, group, 1,
            )
            pieces.append(piece)
            side_value, tied, _ = joined(side_value, tied, piece)
        return pieces, side_value

    relayed = own_pair_of(0)
    window_a = [relayed]
    for _ in range(reach_blocks):
        relayed = shifted(relayed, "ctx", 1)
        window_a.insert(0, relayed)
    window_a = jnp.concatenate(window_a, axis=1)

    window_b = []

    def forward_step(group, relayed_b):
        window_b.insert(0, relayed_b)
        return shifted(relayed_b, "ctx", 1)

    pieces_a, relayed_b = run_chunk(0, window_a, forward_step, own_pair_of(1))
    window_b = jnp.concatenate([relayed_b] + window_b, axis=1)

    def return_step(group, partial):
        if group + 1 < reach_blocks:
            return return_hop(partial, pieces_a, group + 1)
        return shifted(partial, "ctx", -1).astype(jnp.float32)

    pieces_b, arrived_a = run_chunk(1, window_b, return_step, far_payload(pieces_a, 0))

    partial_b = far_payload(pieces_b, 0)
    for block in range(1, reach_blocks):
        partial_b = return_hop(partial_b, pieces_b, block)
    arrived_b = shifted(partial_b, "ctx", -1).astype(jnp.float32)

    query_grad = jnp.concatenate([piece[0] for piece in pieces_a + pieces_b], axis=1)
    key_grads, value_grads = [], []
    for pieces, arrived in ((pieces_a, arrived_a), (pieces_b, arrived_b)):
        key_own = jnp.concatenate([piece[3] for piece in pieces], axis=1)
        value_own = jnp.concatenate([piece[4] for piece in pieces], axis=1)
        key_grads.append((key_own + arrived[0]).astype(jnp.bfloat16))
        value_grads.append((value_own + arrived[1]).astype(jnp.bfloat16))
    return (
        query_grad[None],
        jnp.concatenate(key_grads, axis=1)[None],
        jnp.concatenate(value_grads, axis=1)[None],
    )


def solution(mesh):
    return jax.shard_map(
        local_body,
        mesh=mesh,
        in_specs=(
            P("section", "ctx", None),
            P("section", "ctx", None),
            P("section", "ctx", None),
            P("section", "ctx", None),
            P(),
        ),
        out_specs=(P("section", "ctx", None), P("section", "ctx", None), P("section", "ctx", None)),
        check_vma=False,
    )
```

```python
import jax
import jax.numpy as jnp
from jax import lax
from jax.experimental import pallas as pl
from jax.experimental.pallas import tpu as pltpu
from jax.sharding import PartitionSpec as P


WINDOW = 1024
KV_HEADS = 8
CHUNKS = 2
GROUP = 2


SCORE_SCALE = 168.0 ** (-0.5)


def product(a, b, dims):
    return lax.dot_general(a, b, dims, preferred_element_type=jnp.float32)


def attention_back_kernel(at_ref, q_ref, do_ref, *refs):
    blocks = len(refs) - 7
    piece_refs = refs[:blocks]
    mask_ref = refs[blocks]
    dq_ref, far_ref, own_ref = refs[-3:]
    head_size = piece_refs[0].shape[2]
    heads = q_ref.shape[1] // head_size
    rows = q_ref.shape[0]
    allowed = mask_ref[...] > 0
    keys = jnp.concatenate([ref[0] for ref in piece_refs], axis=0)
    values = jnp.concatenate([ref[1] for ref in piece_refs], axis=0)
    queries = jnp.concatenate([q_ref[:, h * head_size:(h + 1) * head_size] for h in range(heads)], axis=0)
    grads = jnp.concatenate([do_ref[:, h * head_size:(h + 1) * head_size] for h in range(heads)], axis=0)
    allowed = jnp.concatenate([allowed] * heads, axis=0)
    nt = (((1,), (1,)), ((), ()))
    tn = (((0,), (0,)), ((), ()))
    nn = (((1,), (0,)), ((), ()))
    scores = SCORE_SCALE * product(queries, keys, nt)
    scores = jnp.where(allowed, scores, -jnp.inf)
    highest = jnp.max(scores, axis=-1, keepdims=True)
    log_total = highest + jnp.log(jnp.sum(jnp.exp(scores - highest), axis=-1, keepdims=True))
    weights = jnp.exp(scores - log_total)
    weight_half = weights.astype(jnp.bfloat16)
    attended = product(weight_half, values, nn).astype(jnp.bfloat16)
    row_dot = jnp.sum(attended.astype(jnp.float32) * grads.astype(jnp.float32), axis=-1, keepdims=True)
    weight_grad = product(grads, values, nt)
    score_grad = (weights * (weight_grad - row_dot)).astype(jnp.bfloat16)
    query_back = SCORE_SCALE * product(score_grad, keys, nn)
    for h in range(heads):
        dq_ref[:, h * head_size:(h + 1) * head_size] = query_back[h * rows:(h + 1) * rows].astype(dq_ref.dtype)
    key_back = SCORE_SCALE * product(score_grad, queries, tn)
    value_back = product(weight_half, grads, tn)
    for block in range(blocks - 1):
        lines = slice(block * rows, (block + 1) * rows)
        far_ref[block, 0] = key_back[lines].astype(far_ref.dtype)
        far_ref[block, 1] = value_back[lines].astype(far_ref.dtype)
    own_ref[0] = key_back[(blocks - 1) * rows:]
    own_ref[1] = value_back[(blocks - 1) * rows:]


def attention_back(queries, grads, window_pieces, allowed, buffers, query_group, kv_group):
    rows, width = queries.shape
    head_size = width // (GROUP * KV_HEADS)
    group_width = GROUP * head_size
    span = rows * len(window_pieces)
    q_spec = pl.BlockSpec((rows, group_width), lambda g, at: (0, at[0]))
    piece_spec = pl.BlockSpec((2, rows, head_size), lambda g, at: (0, 0, at[1]))
    mask_spec = pl.BlockSpec((rows, span), lambda g, at: (0, 0))
    any_spec = pl.BlockSpec(memory_space=pl.ANY)
    far_spec = pl.BlockSpec((len(window_pieces) - 1, 2, rows, head_size), lambda g, at: (0, 0, 0, at[1]))
    own_spec = pl.BlockSpec((2, rows, head_size), lambda g, at: (0, 0, at[1]))
    inputs = [queries, grads, *window_pieces, allowed, *buffers]
    first_buffer = 1 + len(inputs) - len(buffers)
    grid_spec = pltpu.PrefetchScalarGridSpec(
        num_scalar_prefetch=1,
        grid=(1,),
        in_specs=[q_spec, q_spec] + [piece_spec] * len(window_pieces) + [mask_spec] + [any_spec] * 3,
        out_specs=[q_spec, far_spec, own_spec],
    )
    return pl.pallas_call(
        attention_back_kernel,
        grid_spec=grid_spec,
        out_shape=[jax.ShapeDtypeStruct(b.shape, b.dtype) for b in buffers],
        input_output_aliases={first_buffer + i: i for i in range(3)},
        compiler_params=pltpu.CompilerParams(vmem_limit_bytes=60 * 1024 * 1024),
    )(jnp.array([query_group, kv_group], jnp.int32), *inputs)


def passed_along(shard, axis, by):
    count = lax.axis_size(axis)
    return lax.ppermute(shard, axis, [(i, (i + by) % count) for i in range(count)])


def shifted(value, axis, steps):
    count = lax.axis_size(axis)
    initial, last = (max(0, -steps), min(count, count - steps))
    return lax.ppermute(value, axis, [(source, source + steps) for source in range(initial, last)])


def doc_number(positions, doc_lengths):
    ends = jnp.cumsum(doc_lengths)
    return jnp.sum((positions[:, None] >= ends[None, :]).astype(jnp.int32), axis=1)


def window_mask(query_pos, key_pos, doc_lengths):
    same_doc = (
        doc_number(query_pos, doc_lengths)[:, None] == doc_number(key_pos, doc_lengths)[None, :]
    )
    spacing = query_pos[:, None] - key_pos[None, :]
    return same_doc & (spacing >= 0) & (spacing < WINDOW) & (key_pos[None, :] >= 0)


def local_body(query_rows, key_rows, value_rows, finished_grad, doc_lengths):
    queries = query_rows[0]
    keys_here = key_rows[0]
    values_here = value_rows[0]
    count_rows = queries.shape[0]
    reach_blocks = WINDOW // count_rows
    pair_width = keys_here.shape[1]
    head_size = pair_width // KV_HEADS
    rank_here = lax.axis_index("ctx")
    first_pos = rank_here * count_rows
    arriving = passed_along(finished_grad, "section", -1)[0]
    query_pos = first_pos + jnp.arange(count_rows, dtype=jnp.int32)
    key_pos = first_pos - WINDOW + jnp.arange(WINDOW + count_rows, dtype=jnp.int32)
    allowed = window_mask(query_pos, key_pos, doc_lengths).astype(jnp.float32)
    chunk_groups = KV_HEADS // CHUNKS
    chunk_width = chunk_groups * head_size
    mask = allowed.astype(jnp.bfloat16)

    def own_pair_of(chunk):
        cols = slice(chunk * chunk_width, (chunk + 1) * chunk_width)
        return jnp.stack([keys_here[:, cols], values_here[:, cols]])

    def return_hop(partial, far, block):
        arrived = shifted(partial, "ctx", -1).astype(jnp.float32)
        return (arrived + far[block].astype(jnp.float32)).astype(jnp.bfloat16)

    def run_chunk(chunk, window_pieces, query_back, side_step, side_value):
        far = jnp.zeros((reach_blocks, 2, count_rows, chunk_width), jnp.bfloat16)
        own = jnp.zeros((2, count_rows, chunk_width), jnp.float32)
        for group in range(chunk_groups):
            side_value = side_step(group, side_value)
            query_back, far, own = attention_back(
                queries, arriving, window_pieces, mask, (query_back, far, own),
                chunk * chunk_groups + group, group,
            )
        return query_back, far, own, side_value

    query_back = jnp.zeros(queries.shape, jnp.bfloat16)

    relayed = own_pair_of(0)
    window_a = [relayed]
    for _ in range(reach_blocks):
        relayed = shifted(relayed, "ctx", 1)
        window_a.insert(0, relayed)

    window_b = []

    def forward_step(group, relayed_b):
        window_b.insert(0, relayed_b)
        return shifted(relayed_b, "ctx", 1)

    query_back, far_a, own_a, relayed_b = run_chunk(0, window_a, query_back, forward_step, own_pair_of(1))
    window_b.insert(0, relayed_b)

    def return_step(group, partial):
        if group + 1 < reach_blocks:
            return return_hop(partial, far_a, group + 1)
        return shifted(partial, "ctx", -1).astype(jnp.float32)

    query_back, far_b, own_b, arrived_a = run_chunk(1, window_b, query_back, return_step, far_a[0])

    partial_b = far_b[0]
    for block in range(1, reach_blocks):
        partial_b = return_hop(partial_b, far_b, block)
    arrived_b = shifted(partial_b, "ctx", -1).astype(jnp.float32)

    totals = [(own_a + arrived_a).astype(jnp.bfloat16), (own_b + arrived_b).astype(jnp.bfloat16)]
    return (
        query_back[None],
        jnp.concatenate([total[0] for total in totals], axis=1)[None],
        jnp.concatenate([total[1] for total in totals], axis=1)[None],
    )


def solution(mesh):
    return jax.shard_map(
        local_body,
        mesh=mesh,
        in_specs=(
            P("section", "ctx", None),
            P("section", "ctx", None),
            P("section", "ctx", None),
            P("section", "ctx", None),
            P(),
        ),
        out_specs=(P("section", "ctx", None), P("section", "ctx", None), P("section", "ctx", None)),
        check_vma=False,
    )
```

```python
import jax
import jax.numpy as jnp
from jax import lax
from jax.experimental import pallas as pl
from jax.experimental.pallas import tpu as pltpu
from jax.sharding import PartitionSpec as P


WINDOW = 1024
KV_HEADS = 8
CHUNKS = 4
GROUP = 2


SCORE_SCALE = 168.0 ** (-0.5)


def product(a, b, dims):
    return lax.dot_general(a, b, dims, preferred_element_type=jnp.float32)


def attention_back_kernel(at_ref, q_ref, do_ref, *refs):
    blocks = len(refs) - 7
    piece_refs = refs[:blocks]
    mask_ref = refs[blocks]
    dq_ref, far_ref, own_ref = refs[-3:]
    head_size = piece_refs[0].shape[2]
    heads = q_ref.shape[1] // head_size
    rows = q_ref.shape[0]
    allowed = mask_ref[...] > 0
    keys = jnp.concatenate([ref[0] for ref in piece_refs], axis=0)
    values = jnp.concatenate([ref[1] for ref in piece_refs], axis=0)
    queries = jnp.concatenate([q_ref[:, h * head_size:(h + 1) * head_size] for h in range(heads)], axis=0)
    grads = jnp.concatenate([do_ref[:, h * head_size:(h + 1) * head_size] for h in range(heads)], axis=0)
    allowed = jnp.concatenate([allowed] * heads, axis=0)
    nt = (((1,), (1,)), ((), ()))
    tn = (((0,), (0,)), ((), ()))
    nn = (((1,), (0,)), ((), ()))
    scores = SCORE_SCALE * product(queries, keys, nt)
    scores = jnp.where(allowed, scores, -jnp.inf)
    highest = jnp.max(scores, axis=-1, keepdims=True)
    log_total = highest + jnp.log(jnp.sum(jnp.exp(scores - highest), axis=-1, keepdims=True))
    weights = jnp.exp(scores - log_total)
    weight_half = weights.astype(jnp.bfloat16)
    attended = product(weight_half, values, nn).astype(jnp.bfloat16)
    row_dot = jnp.sum(attended.astype(jnp.float32) * grads.astype(jnp.float32), axis=-1, keepdims=True)
    weight_grad = product(grads, values, nt)
    score_grad = (weights * (weight_grad - row_dot)).astype(jnp.bfloat16)
    query_back = SCORE_SCALE * product(score_grad, keys, nn)
    for h in range(heads):
        dq_ref[:, h * head_size:(h + 1) * head_size] = query_back[h * rows:(h + 1) * rows].astype(dq_ref.dtype)
    key_back = SCORE_SCALE * product(score_grad, queries, tn)
    value_back = product(weight_half, grads, tn)
    for block in range(blocks - 1):
        lines = slice(block * rows, (block + 1) * rows)
        far_ref[block, 0] = key_back[lines].astype(far_ref.dtype)
        far_ref[block, 1] = value_back[lines].astype(far_ref.dtype)
    own_ref[0] = key_back[(blocks - 1) * rows:]
    own_ref[1] = value_back[(blocks - 1) * rows:]


def attention_back(queries, grads, window_pieces, allowed, buffers, query_group, kv_group):
    rows, width = queries.shape
    head_size = width // (GROUP * KV_HEADS)
    group_width = GROUP * head_size
    span = rows * len(window_pieces)
    q_spec = pl.BlockSpec((rows, group_width), lambda g, at: (0, at[0]))
    piece_spec = pl.BlockSpec((2, rows, head_size), lambda g, at: (0, 0, at[1]))
    mask_spec = pl.BlockSpec((rows, span), lambda g, at: (0, 0))
    any_spec = pl.BlockSpec(memory_space=pl.ANY)
    far_spec = pl.BlockSpec((len(window_pieces) - 1, 2, rows, head_size), lambda g, at: (0, 0, 0, at[1]))
    own_spec = pl.BlockSpec((2, rows, head_size), lambda g, at: (0, 0, at[1]))
    inputs = [queries, grads, *window_pieces, allowed, *buffers]
    first_buffer = 1 + len(inputs) - len(buffers)
    grid_spec = pltpu.PrefetchScalarGridSpec(
        num_scalar_prefetch=1,
        grid=(1,),
        in_specs=[q_spec, q_spec] + [piece_spec] * len(window_pieces) + [mask_spec] + [any_spec] * 3,
        out_specs=[q_spec, far_spec, own_spec],
    )
    return pl.pallas_call(
        attention_back_kernel,
        grid_spec=grid_spec,
        out_shape=[jax.ShapeDtypeStruct(b.shape, b.dtype) for b in buffers],
        input_output_aliases={first_buffer + i: i for i in range(3)},
        compiler_params=pltpu.CompilerParams(vmem_limit_bytes=60 * 1024 * 1024),
    )(jnp.array([query_group, kv_group], jnp.int32), *inputs)


def passed_along(shard, axis, by):
    count = lax.axis_size(axis)
    return lax.ppermute(shard, axis, [(i, (i + by) % count) for i in range(count)])


def shifted(value, axis, steps):
    count = lax.axis_size(axis)
    initial, last = (max(0, -steps), min(count, count - steps))
    return lax.ppermute(value, axis, [(source, source + steps) for source in range(initial, last)])


def doc_number(positions, doc_lengths):
    ends = jnp.cumsum(doc_lengths)
    return jnp.sum((positions[:, None] >= ends[None, :]).astype(jnp.int32), axis=1)


def window_mask(query_pos, key_pos, doc_lengths):
    same_doc = (
        doc_number(query_pos, doc_lengths)[:, None] == doc_number(key_pos, doc_lengths)[None, :]
    )
    spacing = query_pos[:, None] - key_pos[None, :]
    return same_doc & (spacing >= 0) & (spacing < WINDOW) & (key_pos[None, :] >= 0)


def local_body(query_rows, key_rows, value_rows, finished_grad, doc_lengths):
    queries = query_rows[0]
    keys_here = key_rows[0]
    values_here = value_rows[0]
    count_rows = queries.shape[0]
    reach_blocks = WINDOW // count_rows
    pair_width = keys_here.shape[1]
    head_size = pair_width // KV_HEADS
    rank_here = lax.axis_index("ctx")
    first_pos = rank_here * count_rows
    arriving = passed_along(finished_grad, "section", -1)[0]
    query_pos = first_pos + jnp.arange(count_rows, dtype=jnp.int32)
    key_pos = first_pos - WINDOW + jnp.arange(WINDOW + count_rows, dtype=jnp.int32)
    allowed = window_mask(query_pos, key_pos, doc_lengths).astype(jnp.float32)
    chunk_groups = KV_HEADS // CHUNKS
    chunk_width = chunk_groups * head_size
    mask = allowed.astype(jnp.bfloat16)

    def own_pair_of(chunk):
        cols = slice(chunk * chunk_width, (chunk + 1) * chunk_width)
        return jnp.stack([keys_here[:, cols], values_here[:, cols]])

    def relay_step(step, state):
        window, relayed = state
        relayed = shifted(relayed, "ctx", 1)
        return [relayed] + window, relayed

    def return_step(step, state):
        far, partial = state
        arrived = shifted(partial, "ctx", -1).astype(jnp.float32)
        if step + 1 < reach_blocks:
            return far, (arrived + far[step + 1].astype(jnp.float32)).astype(jnp.bfloat16)
        return far, arrived

    buffers = {}
    query_back = [jnp.zeros(queries.shape, jnp.bfloat16)]

    def run_pieces(chunks, windows, chains):
        index = 0
        for chunk in chunks:
            far = jnp.zeros((reach_blocks, 2, count_rows, chunk_width), jnp.bfloat16)
            own = jnp.zeros((2, count_rows, chunk_width), jnp.float32)
            for group in range(chunk_groups):
                for name in chains:
                    step_fn, state = chains[name]
                    chains[name] = (step_fn, step_fn(index, state))
                query_back[0], far, own = attention_back(
                    queries, arriving, windows[chunk], mask, (query_back[0], far, own),
                    chunk * chunk_groups + group, group,
                )
                index += 1
            buffers[chunk] = (far, own)
        return {name: chains[name][1] for name in chains}

    half = CHUNKS // 2
    states = {chunk: ([own_pair_of(chunk)], own_pair_of(chunk)) for chunk in range(half)}
    for step in range(reach_blocks):
        for chunk in range(half):
            states[chunk] = relay_step(step, states[chunk])
    windows = {chunk: states[chunk][0] for chunk in range(half)}

    chains = {f"c{chunk}": (relay_step, ([own_pair_of(chunk)], own_pair_of(chunk))) for chunk in range(half, CHUNKS)}
    done = run_pieces(range(half), windows, chains)
    for chunk in range(half, CHUNKS):
        windows[chunk] = done[f"c{chunk}"][0]

    chains = {f"c{chunk}": (return_step, (buffers[chunk][0], buffers[chunk][0][0])) for chunk in range(half)}
    done = run_pieces(range(half, CHUNKS), windows, chains)
    arrived = {chunk: done[f"c{chunk}"][1] for chunk in range(half)}

    states = {chunk: (buffers[chunk][0], buffers[chunk][0][0]) for chunk in range(half, CHUNKS)}
    for step in range(reach_blocks):
        for chunk in range(half, CHUNKS):
            states[chunk] = return_step(step, states[chunk])
    for chunk in range(half, CHUNKS):
        arrived[chunk] = states[chunk][1]

    totals = [(buffers[chunk][1] + arrived[chunk]).astype(jnp.bfloat16) for chunk in range(CHUNKS)]
    return (
        query_back[0][None],
        jnp.concatenate([total[0] for total in totals], axis=1)[None],
        jnp.concatenate([total[1] for total in totals], axis=1)[None],
    )


def solution(mesh):
    return jax.shard_map(
        local_body,
        mesh=mesh,
        in_specs=(
            P("section", "ctx", None),
            P("section", "ctx", None),
            P("section", "ctx", None),
            P("section", "ctx", None),
            P(),
        ),
        out_specs=(P("section", "ctx", None), P("section", "ctx", None), P("section", "ctx", None)),
        check_vma=False,
    )
```

```python
import jax
import jax.numpy as jnp
from jax import lax
from jax.experimental import pallas as pl
from jax.experimental.pallas import tpu as pltpu
from jax.sharding import PartitionSpec as P


WINDOW = 1024
KV_HEADS = 8
CHUNKS = 2
GROUP = 2


SCORE_SCALE = 168.0 ** (-0.5)


def product(a, b, dims):
    return lax.dot_general(a, b, dims, preferred_element_type=jnp.float32)


def attention_back_kernel(at_ref, q_ref, do_ref, *refs):
    blocks = len(refs) - 7
    piece_refs = refs[:blocks]
    mask_ref = refs[blocks]
    dq_ref, far_ref, own_ref = refs[-3:]
    head_size = piece_refs[0].shape[2]
    heads = q_ref.shape[1] // head_size
    rows = q_ref.shape[0]
    allowed = mask_ref[...] > 0
    keys = jnp.concatenate([ref[0] for ref in piece_refs], axis=0)
    values = jnp.concatenate([ref[1] for ref in piece_refs], axis=0)
    queries = jnp.concatenate([q_ref[:, h * head_size:(h + 1) * head_size] for h in range(heads)], axis=0)
    grads = jnp.concatenate([do_ref[:, h * head_size:(h + 1) * head_size] for h in range(heads)], axis=0)
    allowed = jnp.concatenate([allowed] * heads, axis=0)
    nt = (((1,), (1,)), ((), ()))
    tn = (((0,), (0,)), ((), ()))
    nn = (((1,), (0,)), ((), ()))
    scores = SCORE_SCALE * product(queries, keys, nt)
    scores = jnp.where(allowed, scores, -jnp.inf)
    highest = jnp.max(scores, axis=-1, keepdims=True)
    log_total = highest + jnp.log(jnp.sum(jnp.exp(scores - highest), axis=-1, keepdims=True))
    weights = jnp.exp(scores - log_total)
    weight_half = weights.astype(jnp.bfloat16)
    attended = product(weight_half, values, nn).astype(jnp.bfloat16)
    row_dot = jnp.sum(attended.astype(jnp.float32) * grads.astype(jnp.float32), axis=-1, keepdims=True)
    weight_grad = product(grads, values, nt)
    score_grad = (weights * (weight_grad - row_dot)).astype(jnp.bfloat16)
    query_back = SCORE_SCALE * product(score_grad, keys, nn)
    for h in range(heads):
        dq_ref[:, h * head_size:(h + 1) * head_size] = query_back[h * rows:(h + 1) * rows].astype(dq_ref.dtype)
    key_back = SCORE_SCALE * product(score_grad, queries, tn)
    value_back = product(weight_half, grads, tn)
    for block in range(blocks - 1):
        lines = slice(block * rows, (block + 1) * rows)
        far_ref[block, 0] = key_back[lines].astype(far_ref.dtype)
        far_ref[block, 1] = value_back[lines].astype(far_ref.dtype)
    own_ref[0] = key_back[(blocks - 1) * rows:]
    own_ref[1] = value_back[(blocks - 1) * rows:]


def attention_back(queries, grads, window_pieces, allowed, buffers, query_group, kv_group, groups):
    rows, width = queries.shape
    head_size = width // (GROUP * KV_HEADS)
    group_width = GROUP * head_size
    span = rows * len(window_pieces)
    q_spec = pl.BlockSpec((rows, group_width), lambda g, at: (0, g + at[0]))
    piece_spec = pl.BlockSpec((2, rows, head_size), lambda g, at: (0, 0, g + at[1]))
    mask_spec = pl.BlockSpec((rows, span), lambda g, at: (0, 0))
    any_spec = pl.BlockSpec(memory_space=pl.ANY)
    far_spec = pl.BlockSpec((len(window_pieces) - 1, 2, rows, head_size), lambda g, at: (0, 0, 0, g))
    own_spec = pl.BlockSpec((2, rows, head_size), lambda g, at: (0, 0, g))
    inputs = [queries, grads, *window_pieces, allowed, *buffers]
    first_buffer = 1 + len(inputs) - len(buffers)
    grid_spec = pltpu.PrefetchScalarGridSpec(
        num_scalar_prefetch=1,
        grid=(groups,),
        in_specs=[q_spec, q_spec] + [piece_spec] * len(window_pieces) + [mask_spec] + [any_spec] * 3,
        out_specs=[q_spec, far_spec, own_spec],
    )
    return pl.pallas_call(
        attention_back_kernel,
        grid_spec=grid_spec,
        out_shape=[jax.ShapeDtypeStruct(b.shape, b.dtype) for b in buffers],
        input_output_aliases={first_buffer + i: i for i in range(3)},
        compiler_params=pltpu.CompilerParams(vmem_limit_bytes=60 * 1024 * 1024),
    )(jnp.array([query_group, kv_group], jnp.int32), *inputs)


def passed_along(shard, axis, by):
    count = lax.axis_size(axis)
    return lax.ppermute(shard, axis, [(i, (i + by) % count) for i in range(count)])


def shifted(value, axis, steps):
    count = lax.axis_size(axis)
    initial, last = (max(0, -steps), min(count, count - steps))
    return lax.ppermute(value, axis, [(source, source + steps) for source in range(initial, last)])


def doc_number(positions, doc_lengths):
    ends = jnp.cumsum(doc_lengths)
    return jnp.sum((positions[:, None] >= ends[None, :]).astype(jnp.int32), axis=1)


def window_mask(query_pos, key_pos, doc_lengths):
    same_doc = (
        doc_number(query_pos, doc_lengths)[:, None] == doc_number(key_pos, doc_lengths)[None, :]
    )
    spacing = query_pos[:, None] - key_pos[None, :]
    return same_doc & (spacing >= 0) & (spacing < WINDOW) & (key_pos[None, :] >= 0)


def local_body(query_rows, key_rows, value_rows, finished_grad, doc_lengths):
    queries = query_rows[0]
    keys_here = key_rows[0]
    values_here = value_rows[0]
    count_rows = queries.shape[0]
    reach_blocks = WINDOW // count_rows
    pair_width = keys_here.shape[1]
    head_size = pair_width // KV_HEADS
    rank_here = lax.axis_index("ctx")
    first_pos = rank_here * count_rows
    arriving = passed_along(finished_grad, "section", -1)[0]
    query_pos = first_pos + jnp.arange(count_rows, dtype=jnp.int32)
    key_pos = first_pos - WINDOW + jnp.arange(WINDOW + count_rows, dtype=jnp.int32)
    allowed = window_mask(query_pos, key_pos, doc_lengths).astype(jnp.float32)
    chunk_groups = KV_HEADS // CHUNKS
    chunk_width = chunk_groups * head_size
    mask = allowed.astype(jnp.bfloat16)

    def own_pair_of(chunk):
        cols = slice(chunk * chunk_width, (chunk + 1) * chunk_width)
        return jnp.stack([keys_here[:, cols], values_here[:, cols]])

    windows = [[own_pair_of(chunk)] for chunk in range(CHUNKS)]
    for _ in range(reach_blocks):
        for chunk in range(CHUNKS):
            windows[chunk].insert(0, shifted(windows[chunk][0], "ctx", 1))

    query_back = jnp.zeros(queries.shape, jnp.bfloat16)
    results = []
    for chunk in range(CHUNKS):
        far = jnp.zeros((reach_blocks, 2, count_rows, chunk_width), jnp.bfloat16)
        own = jnp.zeros((2, count_rows, chunk_width), jnp.float32)
        query_back, far, own = attention_back(
            queries, arriving, windows[chunk], mask, (query_back, far, own),
            chunk * chunk_groups, 0, chunk_groups,
        )
        results.append((far, own))

    partials = [far[0] for far, _ in results]
    for step in range(reach_blocks):
        for chunk in range(CHUNKS):
            far = results[chunk][0]
            arrived = shifted(partials[chunk], "ctx", -1).astype(jnp.float32)
            if step + 1 < reach_blocks:
                partials[chunk] = (arrived + far[step + 1].astype(jnp.float32)).astype(jnp.bfloat16)
            else:
                partials[chunk] = arrived

    totals = [(own + arrived).astype(jnp.bfloat16) for (_, own), arrived in zip(results, partials)]
    return (
        query_back[None],
        jnp.concatenate([total[0] for total in totals], axis=1)[None],
        jnp.concatenate([total[1] for total in totals], axis=1)[None],
    )


def solution(mesh):
    return jax.shard_map(
        local_body,
        mesh=mesh,
        in_specs=(
            P("section", "ctx", None),
            P("section", "ctx", None),
            P("section", "ctx", None),
            P("section", "ctx", None),
            P(),
        ),
        out_specs=(P("section", "ctx", None), P("section", "ctx", None), P("section", "ctx", None)),
        check_vma=False,
    )
```

```python
import jax
import jax.numpy as jnp
from jax import lax
from jax.experimental import pallas as pl
from jax.experimental.pallas import tpu as pltpu
from jax.sharding import PartitionSpec as P


WINDOW = 1024
KV_HEADS = 8
CHUNKS = 2
GROUP = 2


SCORE_SCALE = 168.0 ** (-0.5)


def product(a, b, dims):
    return lax.dot_general(a, b, dims, preferred_element_type=jnp.float32)


def attention_back_kernel(at_ref, q_ref, do_ref, *refs):
    blocks = len(refs) - 4
    piece_refs = refs[:blocks]
    mask_ref = refs[blocks]
    dq_ref, far_ref, own_ref = refs[-3:]
    head_size = piece_refs[0].shape[2]
    heads = q_ref.shape[1] // head_size
    rows = q_ref.shape[0]
    allowed = mask_ref[...] > 0
    keys = jnp.concatenate([ref[0] for ref in piece_refs], axis=0)
    values = jnp.concatenate([ref[1] for ref in piece_refs], axis=0)
    queries = jnp.concatenate([q_ref[:, h * head_size:(h + 1) * head_size] for h in range(heads)], axis=0)
    grads = jnp.concatenate([do_ref[:, h * head_size:(h + 1) * head_size] for h in range(heads)], axis=0)
    allowed = jnp.concatenate([allowed] * heads, axis=0)
    nt = (((1,), (1,)), ((), ()))
    tn = (((0,), (0,)), ((), ()))
    nn = (((1,), (0,)), ((), ()))
    scores = SCORE_SCALE * product(queries, keys, nt)
    scores = jnp.where(allowed, scores, -jnp.inf)
    highest = jnp.max(scores, axis=-1, keepdims=True)
    shifted_exp = jnp.exp(scores - highest)
    weights = shifted_exp * (1.0 / jnp.sum(shifted_exp, axis=-1, keepdims=True))
    weight_half = weights.astype(jnp.bfloat16)
    attended = product(weight_half, values, nn).astype(jnp.bfloat16)
    row_dot = jnp.sum(attended.astype(jnp.float32) * grads.astype(jnp.float32), axis=-1, keepdims=True)
    weight_grad = product(grads, values, nt)
    score_grad = (weights * (weight_grad - row_dot)).astype(jnp.bfloat16)
    query_back = SCORE_SCALE * product(score_grad, keys, nn)
    for h in range(heads):
        dq_ref[:, h * head_size:(h + 1) * head_size] = query_back[h * rows:(h + 1) * rows].astype(dq_ref.dtype)
    key_back = SCORE_SCALE * product(score_grad, queries, tn)
    value_back = product(weight_half, grads, tn)
    for block in range(blocks - 1):
        lines = slice(block * rows, (block + 1) * rows)
        far_ref[block, 0] = key_back[lines].astype(far_ref.dtype)
        far_ref[block, 1] = value_back[lines].astype(far_ref.dtype)
    own_ref[0] = key_back[(blocks - 1) * rows:]
    own_ref[1] = value_back[(blocks - 1) * rows:]


def attention_back(queries, grads, window_pieces, allowed, query_group, kv_group, groups):
    rows, width = queries.shape
    head_size = width // (GROUP * KV_HEADS)
    group_width = GROUP * head_size
    span = rows * len(window_pieces)
    q_spec = pl.BlockSpec((rows, group_width), lambda g, at: (0, g + at[0]))
    piece_spec = pl.BlockSpec((2, rows, head_size), lambda g, at: (0, 0, g + at[1]))
    mask_spec = pl.BlockSpec((rows, span), lambda g, at: (0, 0))
    far_spec = pl.BlockSpec((len(window_pieces) - 1, 2, rows, head_size), lambda g, at: (0, 0, 0, g))
    own_spec = pl.BlockSpec((2, rows, head_size), lambda g, at: (0, 0, g))
    inputs = [queries, grads, *window_pieces, allowed]
    dq_spec = pl.BlockSpec((rows, group_width), lambda g, at: (0, g))
    grid_spec = pltpu.PrefetchScalarGridSpec(
        num_scalar_prefetch=1,
        grid=(groups,),
        in_specs=[q_spec, q_spec] + [piece_spec] * len(window_pieces) + [mask_spec],
        out_specs=[dq_spec, far_spec, own_spec],
    )
    chunk_width = groups * head_size
    return pl.pallas_call(
        attention_back_kernel,
        grid_spec=grid_spec,
        out_shape=[
            jax.ShapeDtypeStruct((rows, groups * group_width), jnp.bfloat16),
            jax.ShapeDtypeStruct((len(window_pieces) - 1, 2, rows, chunk_width), jnp.bfloat16),
            jax.ShapeDtypeStruct((2, rows, chunk_width), jnp.float32),
        ],
        compiler_params=pltpu.CompilerParams(vmem_limit_bytes=60 * 1024 * 1024),
    )(jnp.array([query_group, kv_group], jnp.int32), *inputs)


def passed_along(shard, axis, by):
    count = lax.axis_size(axis)
    return lax.ppermute(shard, axis, [(i, (i + by) % count) for i in range(count)])


def shifted(value, axis, steps):
    count = lax.axis_size(axis)
    initial, last = (max(0, -steps), min(count, count - steps))
    return lax.ppermute(value, axis, [(source, source + steps) for source in range(initial, last)])


def doc_number(positions, doc_lengths):
    ends = jnp.cumsum(doc_lengths)
    return jnp.sum((positions[:, None] >= ends[None, :]).astype(jnp.int32), axis=1)


def window_mask(query_pos, key_pos, doc_lengths):
    same_doc = (
        doc_number(query_pos, doc_lengths)[:, None] == doc_number(key_pos, doc_lengths)[None, :]
    )
    spacing = query_pos[:, None] - key_pos[None, :]
    return same_doc & (spacing >= 0) & (spacing < WINDOW) & (key_pos[None, :] >= 0)


def local_body(query_rows, key_rows, value_rows, finished_grad, doc_lengths):
    queries = query_rows[0]
    keys_here = key_rows[0]
    values_here = value_rows[0]
    count_rows = queries.shape[0]
    reach_blocks = WINDOW // count_rows
    pair_width = keys_here.shape[1]
    head_size = pair_width // KV_HEADS
    rank_here = lax.axis_index("ctx")
    first_pos = rank_here * count_rows
    arriving = passed_along(finished_grad, "section", -1)[0]
    query_pos = first_pos + jnp.arange(count_rows, dtype=jnp.int32)
    key_pos = first_pos - WINDOW + jnp.arange(WINDOW + count_rows, dtype=jnp.int32)
    allowed = window_mask(query_pos, key_pos, doc_lengths).astype(jnp.float32)
    chunk_groups = KV_HEADS // CHUNKS
    chunk_width = chunk_groups * head_size
    mask = allowed.astype(jnp.bfloat16)

    def own_pair_of(chunk):
        cols = slice(chunk * chunk_width, (chunk + 1) * chunk_width)
        return jnp.stack([keys_here[:, cols], values_here[:, cols]])

    windows = [[own_pair_of(chunk)] for chunk in range(CHUNKS)]
    for _ in range(reach_blocks):
        for chunk in range(CHUNKS):
            windows[chunk].insert(0, shifted(windows[chunk][0], "ctx", 1))

    query_parts = []
    results = []
    for chunk in range(CHUNKS):
        query_part, far, own = attention_back(
            queries, arriving, windows[chunk], mask, chunk * chunk_groups, 0, chunk_groups
        )
        query_parts.append(query_part)
        results.append((far, own))
    query_back = jnp.concatenate(query_parts, axis=1)

    partials = [far[0] for far, _ in results]
    for step in range(reach_blocks):
        for chunk in range(CHUNKS):
            far = results[chunk][0]
            arrived = shifted(partials[chunk], "ctx", -1).astype(jnp.float32)
            if step + 1 < reach_blocks:
                partials[chunk] = (arrived + far[step + 1].astype(jnp.float32)).astype(jnp.bfloat16)
            else:
                partials[chunk] = arrived

    totals = [(own + arrived).astype(jnp.bfloat16) for (_, own), arrived in zip(results, partials)]
    return (
        query_back[None],
        jnp.concatenate([total[0] for total in totals], axis=1)[None],
        jnp.concatenate([total[1] for total in totals], axis=1)[None],
    )


def solution(mesh):
    return jax.shard_map(
        local_body,
        mesh=mesh,
        in_specs=(
            P("section", "ctx", None),
            P("section", "ctx", None),
            P("section", "ctx", None),
            P("section", "ctx", None),
            P(),
        ),
        out_specs=(P("section", "ctx", None), P("section", "ctx", None), P("section", "ctx", None)),
        check_vma=False,
    )
```

```python
import jax
import jax.numpy as jnp
from jax import lax
from jax.experimental import pallas as pl
from jax.experimental.pallas import tpu as pltpu
from jax.sharding import PartitionSpec as P


WINDOW = 1024
KV_HEADS = 8
CHUNKS = 2
GROUP = 2


SCORE_SCALE = 168.0 ** (-0.5)


def product(a, b, dims):
    return lax.dot_general(a, b, dims, preferred_element_type=jnp.float32)


def attention_back_kernel(at_ref, q_ref, do_ref, *refs):
    blocks = len(refs) - 4
    piece_refs = refs[:blocks]
    mask_ref = refs[blocks]
    dq_ref, far_ref, own_ref = refs[-3:]
    head_size = piece_refs[0].shape[2]
    heads = q_ref.shape[1] // head_size
    rows = q_ref.shape[0]
    allowed = mask_ref[...] > 0
    keys = jnp.concatenate([ref[0] for ref in piece_refs], axis=0)
    values = jnp.concatenate([ref[1] for ref in piece_refs], axis=0)
    queries = jnp.concatenate([q_ref[:, h * head_size:(h + 1) * head_size] for h in range(heads)], axis=0)
    grads = jnp.concatenate([do_ref[:, h * head_size:(h + 1) * head_size] for h in range(heads)], axis=0)
    allowed = jnp.concatenate([allowed] * heads, axis=0)
    nt = (((1,), (1,)), ((), ()))
    nn = (((1,), (0,)), ((), ()))
    scores = SCORE_SCALE * product(queries, keys, nt)
    scores = jnp.where(allowed, scores, -jnp.inf)
    highest = jnp.max(scores, axis=-1, keepdims=True)
    shifted_exp = jnp.exp(scores - highest)
    weights = shifted_exp * (1.0 / jnp.sum(shifted_exp, axis=-1, keepdims=True))
    weight_half = weights.astype(jnp.bfloat16)
    attended = product(weight_half, values, nn).astype(jnp.bfloat16)
    row_dot = jnp.sum(attended.astype(jnp.float32) * grads.astype(jnp.float32), axis=-1, keepdims=True)
    weight_grad = product(grads, values, nt)
    score_grad = (weights * (weight_grad - row_dot)).astype(jnp.bfloat16)
    query_back = SCORE_SCALE * product(score_grad, keys, nn)
    for h in range(heads):
        dq_ref[:, h * head_size:(h + 1) * head_size] = query_back[h * rows:(h + 1) * rows].astype(dq_ref.dtype)
    key_back = (SCORE_SCALE * product(queries.T, score_grad, nn)).T
    value_back = product(grads.T, weight_half, nn).T
    for block in range(blocks - 1):
        lines = slice(block * rows, (block + 1) * rows)
        far_ref[block, 0] = key_back[lines].astype(far_ref.dtype)
        far_ref[block, 1] = value_back[lines].astype(far_ref.dtype)
    own_ref[0] = key_back[(blocks - 1) * rows:]
    own_ref[1] = value_back[(blocks - 1) * rows:]


def attention_back(queries, grads, window_pieces, allowed, query_group, kv_group, groups):
    rows, width = queries.shape
    head_size = width // (GROUP * KV_HEADS)
    group_width = GROUP * head_size
    span = rows * len(window_pieces)
    q_spec = pl.BlockSpec((rows, group_width), lambda g, at: (0, g + at[0]))
    piece_spec = pl.BlockSpec((2, rows, head_size), lambda g, at: (0, 0, g + at[1]))
    mask_spec = pl.BlockSpec((rows, span), lambda g, at: (0, 0))
    far_spec = pl.BlockSpec((len(window_pieces) - 1, 2, rows, head_size), lambda g, at: (0, 0, 0, g))
    own_spec = pl.BlockSpec((2, rows, head_size), lambda g, at: (0, 0, g))
    inputs = [queries, grads, *window_pieces, allowed]
    dq_spec = pl.BlockSpec((rows, group_width), lambda g, at: (0, g))
    grid_spec = pltpu.PrefetchScalarGridSpec(
        num_scalar_prefetch=1,
        grid=(groups,),
        in_specs=[q_spec, q_spec] + [piece_spec] * len(window_pieces) + [mask_spec],
        out_specs=[dq_spec, far_spec, own_spec],
    )
    chunk_width = groups * head_size
    return pl.pallas_call(
        attention_back_kernel,
        grid_spec=grid_spec,
        out_shape=[
            jax.ShapeDtypeStruct((rows, groups * group_width), jnp.bfloat16),
            jax.ShapeDtypeStruct((len(window_pieces) - 1, 2, rows, chunk_width), jnp.bfloat16),
            jax.ShapeDtypeStruct((2, rows, chunk_width), jnp.float32),
        ],
        compiler_params=pltpu.CompilerParams(vmem_limit_bytes=60 * 1024 * 1024),
    )(jnp.array([query_group, kv_group], jnp.int32), *inputs)


def passed_along(shard, axis, by):
    count = lax.axis_size(axis)
    return lax.ppermute(shard, axis, [(i, (i + by) % count) for i in range(count)])


def shifted(value, axis, steps):
    count = lax.axis_size(axis)
    initial, last = (max(0, -steps), min(count, count - steps))
    return lax.ppermute(value, axis, [(source, source + steps) for source in range(initial, last)])


def doc_number(positions, doc_lengths):
    ends = jnp.cumsum(doc_lengths)
    return jnp.sum((positions[:, None] >= ends[None, :]).astype(jnp.int32), axis=1)


def window_mask(query_pos, key_pos, doc_lengths):
    same_doc = (
        doc_number(query_pos, doc_lengths)[:, None] == doc_number(key_pos, doc_lengths)[None, :]
    )
    spacing = query_pos[:, None] - key_pos[None, :]
    return same_doc & (spacing >= 0) & (spacing < WINDOW) & (key_pos[None, :] >= 0)


def local_body(query_rows, key_rows, value_rows, finished_grad, doc_lengths):
    queries = query_rows[0]
    keys_here = key_rows[0]
    values_here = value_rows[0]
    count_rows = queries.shape[0]
    reach_blocks = WINDOW // count_rows
    pair_width = keys_here.shape[1]
    head_size = pair_width // KV_HEADS
    rank_here = lax.axis_index("ctx")
    first_pos = rank_here * count_rows
    arriving = passed_along(finished_grad, "section", -1)[0]
    query_pos = first_pos + jnp.arange(count_rows, dtype=jnp.int32)
    key_pos = first_pos - WINDOW + jnp.arange(WINDOW + count_rows, dtype=jnp.int32)
    allowed = window_mask(query_pos, key_pos, doc_lengths).astype(jnp.float32)
    chunk_groups = KV_HEADS // CHUNKS
    chunk_width = chunk_groups * head_size
    mask = allowed.astype(jnp.bfloat16)

    def own_pair_of(chunk):
        cols = slice(chunk * chunk_width, (chunk + 1) * chunk_width)
        return jnp.stack([keys_here[:, cols], values_here[:, cols]])

    windows = [[own_pair_of(chunk)] for chunk in range(CHUNKS)]
    for _ in range(reach_blocks):
        for chunk in range(CHUNKS):
            windows[chunk].insert(0, shifted(windows[chunk][0], "ctx", 1))

    query_parts = []
    results = []
    for chunk in range(CHUNKS):
        query_part, far, own = attention_back(
            queries, arriving, windows[chunk], mask, chunk * chunk_groups, 0, chunk_groups
        )
        query_parts.append(query_part)
        results.append((far, own))
    query_back = jnp.concatenate(query_parts, axis=1)

    partials = [far[0] for far, _ in results]
    for step in range(reach_blocks):
        for chunk in range(CHUNKS):
            far = results[chunk][0]
            arrived = shifted(partials[chunk], "ctx", -1).astype(jnp.float32)
            if step + 1 < reach_blocks:
                partials[chunk] = (arrived + far[step + 1].astype(jnp.float32)).astype(jnp.bfloat16)
            else:
                partials[chunk] = arrived

    totals = [(own + arrived).astype(jnp.bfloat16) for (_, own), arrived in zip(results, partials)]
    return (
        query_back[None],
        jnp.concatenate([total[0] for total in totals], axis=1)[None],
        jnp.concatenate([total[1] for total in totals], axis=1)[None],
    )


def solution(mesh):
    return jax.shard_map(
        local_body,
        mesh=mesh,
        in_specs=(
            P("section", "ctx", None),
            P("section", "ctx", None),
            P("section", "ctx", None),
            P("section", "ctx", None),
            P(),
        ),
        out_specs=(P("section", "ctx", None), P("section", "ctx", None), P("section", "ctx", None)),
        check_vma=False,
    )
```

```python
import jax
import jax.numpy as jnp
from jax import lax
from jax.experimental import pallas as pl
from jax.experimental.pallas import tpu as pltpu
from jax.sharding import PartitionSpec as P


WINDOW = 1024
KV_HEADS = 8
CHUNK_GROUPS = (5, 3)
GROUP = 2


SCORE_SCALE = 168.0 ** (-0.5)


def product(a, b, dims):
    return lax.dot_general(a, b, dims, preferred_element_type=jnp.float32)


def attention_back_kernel(at_ref, q_ref, do_ref, *refs):
    blocks = len(refs) - 4
    piece_refs = refs[:blocks]
    mask_ref = refs[blocks]
    dq_ref, far_ref, own_ref = refs[-3:]
    head_size = piece_refs[0].shape[2]
    heads = q_ref.shape[1] // head_size
    rows = q_ref.shape[0]
    allowed = mask_ref[...] > 0
    keys = jnp.concatenate([ref[0] for ref in piece_refs], axis=0)
    values = jnp.concatenate([ref[1] for ref in piece_refs], axis=0)
    queries = jnp.concatenate([q_ref[:, h * head_size:(h + 1) * head_size] for h in range(heads)], axis=0)
    grads = jnp.concatenate([do_ref[:, h * head_size:(h + 1) * head_size] for h in range(heads)], axis=0)
    allowed = jnp.concatenate([allowed] * heads, axis=0)
    nt = (((1,), (1,)), ((), ()))
    nn = (((1,), (0,)), ((), ()))
    scores = SCORE_SCALE * product(queries, keys, nt)
    scores = jnp.where(allowed, scores, -jnp.inf)
    highest = jnp.max(scores, axis=-1, keepdims=True)
    shifted_exp = jnp.exp(scores - highest)
    weights = shifted_exp * (1.0 / jnp.sum(shifted_exp, axis=-1, keepdims=True))
    weight_half = weights.astype(jnp.bfloat16)
    attended = product(weight_half, values, nn).astype(jnp.bfloat16)
    row_dot = jnp.sum(attended.astype(jnp.float32) * grads.astype(jnp.float32), axis=-1, keepdims=True)
    weight_grad = product(grads, values, nt)
    score_grad = (weights * (weight_grad - row_dot)).astype(jnp.bfloat16)
    query_back = SCORE_SCALE * product(score_grad, keys, nn)
    for h in range(heads):
        dq_ref[:, h * head_size:(h + 1) * head_size] = query_back[h * rows:(h + 1) * rows].astype(dq_ref.dtype)
    key_back = (SCORE_SCALE * product(queries.T, score_grad, nn)).T
    value_back = product(grads.T, weight_half, nn).T
    for block in range(blocks - 1):
        lines = slice(block * rows, (block + 1) * rows)
        far_ref[block, 0] = key_back[lines].astype(far_ref.dtype)
        far_ref[block, 1] = value_back[lines].astype(far_ref.dtype)
    own_ref[0] = key_back[(blocks - 1) * rows:]
    own_ref[1] = value_back[(blocks - 1) * rows:]


def attention_back(queries, grads, window_pieces, allowed, query_group, kv_group, groups):
    rows, width = queries.shape
    head_size = width // (GROUP * KV_HEADS)
    group_width = GROUP * head_size
    span = rows * len(window_pieces)
    q_spec = pl.BlockSpec((rows, group_width), lambda g, at: (0, g + at[0]))
    piece_spec = pl.BlockSpec((2, rows, head_size), lambda g, at: (0, 0, g + at[1]))
    mask_spec = pl.BlockSpec((rows, span), lambda g, at: (0, 0))
    far_spec = pl.BlockSpec((len(window_pieces) - 1, 2, rows, head_size), lambda g, at: (0, 0, 0, g))
    own_spec = pl.BlockSpec((2, rows, head_size), lambda g, at: (0, 0, g))
    inputs = [queries, grads, *window_pieces, allowed]
    dq_spec = pl.BlockSpec((rows, group_width), lambda g, at: (0, g))
    grid_spec = pltpu.PrefetchScalarGridSpec(
        num_scalar_prefetch=1,
        grid=(groups,),
        in_specs=[q_spec, q_spec] + [piece_spec] * len(window_pieces) + [mask_spec],
        out_specs=[dq_spec, far_spec, own_spec],
    )
    chunk_width = groups * head_size
    return pl.pallas_call(
        attention_back_kernel,
        grid_spec=grid_spec,
        out_shape=[
            jax.ShapeDtypeStruct((rows, groups * group_width), jnp.bfloat16),
            jax.ShapeDtypeStruct((len(window_pieces) - 1, 2, rows, chunk_width), jnp.bfloat16),
            jax.ShapeDtypeStruct((2, rows, chunk_width), jnp.float32),
        ],
        compiler_params=pltpu.CompilerParams(vmem_limit_bytes=60 * 1024 * 1024),
    )(jnp.array([query_group, kv_group], jnp.int32), *inputs)


def passed_along(shard, axis, by):
    count = lax.axis_size(axis)
    return lax.ppermute(shard, axis, [(i, (i + by) % count) for i in range(count)])


def shifted(value, axis, steps):
    count = lax.axis_size(axis)
    initial, last = (max(0, -steps), min(count, count - steps))
    return lax.ppermute(value, axis, [(source, source + steps) for source in range(initial, last)])


def doc_number(positions, doc_lengths):
    ends = jnp.cumsum(doc_lengths)
    return jnp.sum((positions[:, None] >= ends[None, :]).astype(jnp.int32), axis=1)


def window_mask(query_pos, key_pos, doc_lengths):
    same_doc = (
        doc_number(query_pos, doc_lengths)[:, None] == doc_number(key_pos, doc_lengths)[None, :]
    )
    spacing = query_pos[:, None] - key_pos[None, :]
    return same_doc & (spacing >= 0) & (spacing < WINDOW) & (key_pos[None, :] >= 0)


def local_body(query_rows, key_rows, value_rows, finished_grad, doc_lengths):
    queries = query_rows[0]
    keys_here = key_rows[0]
    values_here = value_rows[0]
    count_rows = queries.shape[0]
    pair_width = keys_here.shape[1]
    head_size = pair_width // KV_HEADS
    rank_here = lax.axis_index("ctx")
    first_pos = rank_here * count_rows
    arriving = passed_along(finished_grad, "section", -1)[0]
    query_pos = first_pos + jnp.arange(count_rows, dtype=jnp.int32)
    key_pos = first_pos - WINDOW + jnp.arange(WINDOW + count_rows, dtype=jnp.int32)
    allowed = window_mask(query_pos, key_pos, doc_lengths).astype(jnp.float32)
    mask = allowed.astype(jnp.bfloat16)

    odd = (rank_here % 2) == 1

    def partner(value):
        count = lax.axis_size("ctx")
        return lax.ppermute(value, "ctx", [(i, i ^ 1) for i in range(count)])

    def forward(own):
        minus_two = shifted(own, "ctx", 2)
        minus_one = partner(jnp.where(odd, minus_two, own))
        minus_four = shifted(minus_two, "ctx", 2)
        minus_three = partner(jnp.where(odd, minus_four, minus_two))
        return [minus_four, minus_three, minus_two, minus_one, own]

    def backward(far, own):
        passed = partner(jnp.stack([far[3], far[1]])).astype(jnp.float32)
        zero = jnp.zeros_like(passed[0])
        to_four = far[0].astype(jnp.float32) + jnp.where(odd, passed[1], zero)
        to_two = far[2].astype(jnp.float32) + jnp.where(odd, passed[0], passed[1])
        direct = jnp.where(odd, zero, passed[0])
        arrived = shifted(to_four.astype(jnp.bfloat16), "ctx", -2).astype(jnp.float32)
        arrived = shifted((arrived + to_two).astype(jnp.bfloat16), "ctx", -2).astype(jnp.float32)
        return (own + (arrived + direct)).astype(jnp.bfloat16)

    firsts = [sum(CHUNK_GROUPS[:chunk]) for chunk in range(len(CHUNK_GROUPS))]
    query_parts = []
    totals = []
    windows = []
    after = None
    for chunk, groups in enumerate(CHUNK_GROUPS):
        cols = slice(firsts[chunk] * head_size, (firsts[chunk] + groups) * head_size)
        own_pair = jnp.stack([keys_here[:, cols], values_here[:, cols]])
        if after is not None:
            own_pair = lax.optimization_barrier((own_pair, after))[0]
        windows.append(forward(own_pair))
        after = windows[-1][0]
    for chunk, groups in enumerate(CHUNK_GROUPS):
        query_part, far, own = attention_back(
            queries, arriving, windows[chunk], mask, firsts[chunk], 0, groups
        )
        query_parts.append(query_part)
        totals.append(backward(far, own))
    query_back = jnp.concatenate(query_parts, axis=1)

    return (
        query_back[None],
        jnp.concatenate([total[0] for total in totals], axis=1)[None],
        jnp.concatenate([total[1] for total in totals], axis=1)[None],
    )


def solution(mesh):
    return jax.shard_map(
        local_body,
        mesh=mesh,
        in_specs=(
            P("section", "ctx", None),
            P("section", "ctx", None),
            P("section", "ctx", None),
            P("section", "ctx", None),
            P(),
        ),
        out_specs=(P("section", "ctx", None), P("section", "ctx", None), P("section", "ctx", None)),
        check_vma=False,
    )
```

```python
import jax
import jax.numpy as jnp
from jax import lax
from jax.experimental import pallas as pl
from jax.experimental.pallas import tpu as pltpu
from jax.sharding import PartitionSpec as P


WINDOW = 1024
KV_HEADS = 8
CHUNKS = 2
GROUP = 2


SCORE_SCALE = 168.0 ** (-0.5)


def product(a, b, dims):
    return lax.dot_general(a, b, dims, preferred_element_type=jnp.float32)


def attention_back_kernel(at_ref, q_ref, do_ref, *refs):
    blocks = (len(refs) - 4) // 2
    key_refs = refs[:blocks]
    value_refs = refs[blocks:2 * blocks]
    mask_ref = refs[2 * blocks]
    dq_ref, far_ref, own_ref = refs[-3:]
    head_size = key_refs[0].shape[1]
    heads = q_ref.shape[1] // head_size
    rows = q_ref.shape[0]
    allowed = mask_ref[...] > 0
    keys = jnp.concatenate([ref[...] for ref in key_refs], axis=0)
    values = jnp.concatenate([ref[...] for ref in value_refs], axis=0)
    queries = jnp.concatenate([q_ref[:, h * head_size:(h + 1) * head_size] for h in range(heads)], axis=0)
    grads = jnp.concatenate([do_ref[:, h * head_size:(h + 1) * head_size] for h in range(heads)], axis=0)
    allowed = jnp.concatenate([allowed] * heads, axis=0)
    nt = (((1,), (1,)), ((), ()))
    nn = (((1,), (0,)), ((), ()))
    scores = SCORE_SCALE * product(queries, keys, nt)
    scores = jnp.where(allowed, scores, -jnp.inf)
    highest = jnp.max(scores, axis=-1, keepdims=True)
    shifted_exp = jnp.exp(scores - highest)
    weights = shifted_exp * (1.0 / jnp.sum(shifted_exp, axis=-1, keepdims=True))
    weight_half = weights.astype(jnp.bfloat16)
    attended = product(weight_half, values, nn).astype(jnp.bfloat16)
    row_dot = jnp.sum(attended.astype(jnp.float32) * grads.astype(jnp.float32), axis=-1, keepdims=True)
    weight_grad = product(grads, values, nt)
    score_grad = (weights * (weight_grad - row_dot)).astype(jnp.bfloat16)
    query_back = SCORE_SCALE * product(score_grad, keys, nn)
    for h in range(heads):
        dq_ref[:, h * head_size:(h + 1) * head_size] = query_back[h * rows:(h + 1) * rows].astype(dq_ref.dtype)
    key_back = (SCORE_SCALE * product(queries.T, score_grad, nn)).T
    value_back = product(grads.T, weight_half, nn).T
    for block in range(blocks - 1):
        lines = slice(block * rows, (block + 1) * rows)
        far_ref[block, 0] = key_back[lines].astype(far_ref.dtype)
        far_ref[block, 1] = value_back[lines].astype(far_ref.dtype)
    own_ref[0] = key_back[(blocks - 1) * rows:]
    own_ref[1] = value_back[(blocks - 1) * rows:]


def attention_back(queries, grads, key_pieces, value_pieces, allowed, query_group, kv_group, groups):
    window_pieces = key_pieces
    rows, width = queries.shape
    head_size = width // (GROUP * KV_HEADS)
    group_width = GROUP * head_size
    span = rows * len(window_pieces)
    q_spec = pl.BlockSpec((rows, group_width), lambda g, at: (0, g + at[0]))
    piece_spec = pl.BlockSpec((rows, head_size), lambda g, at: (0, g + at[1]))
    mask_spec = pl.BlockSpec((rows, span), lambda g, at: (0, 0))
    far_spec = pl.BlockSpec((len(window_pieces) - 1, 2, rows, head_size), lambda g, at: (0, 0, 0, g))
    own_spec = pl.BlockSpec((2, rows, head_size), lambda g, at: (0, 0, g))
    inputs = [queries, grads, *key_pieces, *value_pieces, allowed]
    dq_spec = pl.BlockSpec((rows, group_width), lambda g, at: (0, g))
    grid_spec = pltpu.PrefetchScalarGridSpec(
        num_scalar_prefetch=1,
        grid=(groups,),
        in_specs=[q_spec, q_spec] + [piece_spec] * (2 * len(window_pieces)) + [mask_spec],
        out_specs=[dq_spec, far_spec, own_spec],
    )
    chunk_width = groups * head_size
    return pl.pallas_call(
        attention_back_kernel,
        grid_spec=grid_spec,
        out_shape=[
            jax.ShapeDtypeStruct((rows, groups * group_width), jnp.bfloat16),
            jax.ShapeDtypeStruct((len(window_pieces) - 1, 2, rows, chunk_width), jnp.bfloat16),
            jax.ShapeDtypeStruct((2, rows, chunk_width), jnp.float32),
        ],
        compiler_params=pltpu.CompilerParams(vmem_limit_bytes=60 * 1024 * 1024),
    )(jnp.array([query_group, kv_group], jnp.int32), *inputs)


def passed_along(shard, axis, by):
    count = lax.axis_size(axis)
    return lax.ppermute(shard, axis, [(i, (i + by) % count) for i in range(count)])


def shifted(value, axis, steps):
    count = lax.axis_size(axis)
    initial, last = (max(0, -steps), min(count, count - steps))
    return lax.ppermute(value, axis, [(source, source + steps) for source in range(initial, last)])


def doc_number(positions, doc_lengths):
    ends = jnp.cumsum(doc_lengths)
    return jnp.sum((positions[:, None] >= ends[None, :]).astype(jnp.int32), axis=1)


def window_mask(query_pos, key_pos, doc_lengths):
    same_doc = (
        doc_number(query_pos, doc_lengths)[:, None] == doc_number(key_pos, doc_lengths)[None, :]
    )
    spacing = query_pos[:, None] - key_pos[None, :]
    return same_doc & (spacing >= 0) & (spacing < WINDOW) & (key_pos[None, :] >= 0)


def local_body(query_rows, key_rows, value_rows, finished_grad, doc_lengths):
    queries = query_rows[0]
    keys_here = key_rows[0]
    values_here = value_rows[0]
    count_rows = queries.shape[0]
    pair_width = keys_here.shape[1]
    head_size = pair_width // KV_HEADS
    rank_here = lax.axis_index("ctx")
    first_pos = rank_here * count_rows
    arriving = passed_along(finished_grad, "section", -1)[0]
    query_pos = first_pos + jnp.arange(count_rows, dtype=jnp.int32)
    key_pos = first_pos - WINDOW + jnp.arange(WINDOW + count_rows, dtype=jnp.int32)
    allowed = window_mask(query_pos, key_pos, doc_lengths).astype(jnp.float32)
    chunk_groups = KV_HEADS // CHUNKS
    chunk_width = chunk_groups * head_size
    mask = allowed.astype(jnp.bfloat16)

    def own_pair_of(chunk):
        cols = slice(chunk * chunk_width, (chunk + 1) * chunk_width)
        return [keys_here[:, cols], values_here[:, cols]]

    odd = (rank_here % 2) == 1

    def partner(value):
        count = lax.axis_size("ctx")
        return lax.ppermute(value, "ctx", [(i, i ^ 1) for i in range(count)])

    def forward(own):
        minus_two = [shifted(half, "ctx", 2) for half in own]
        minus_one = [partner(jnp.where(odd, a, b)) for a, b in zip(minus_two, own)]
        minus_four = [shifted(half, "ctx", 2) for half in minus_two]
        minus_three = [partner(jnp.where(odd, a, b)) for a, b in zip(minus_four, minus_two)]
        return [minus_four, minus_three, minus_two, minus_one, own]

    def backward(far, own):
        passed = [partner(jnp.stack([far[3, h], far[1, h]])).astype(jnp.float32) for h in range(2)]
        to_four, to_two, direct = [], [], []
        for h in range(2):
            zero = jnp.zeros_like(passed[h][0])
            to_four.append(far[0, h].astype(jnp.float32) + jnp.where(odd, passed[h][1], zero))
            to_two.append(far[2, h].astype(jnp.float32) + jnp.where(odd, passed[h][0], passed[h][1]))
            direct.append(jnp.where(odd, zero, passed[h][0]))
        arrived = [shifted(x.astype(jnp.bfloat16), "ctx", -2).astype(jnp.float32) for x in to_four]
        arrived = [
            shifted((a + t).astype(jnp.bfloat16), "ctx", -2).astype(jnp.float32)
            for a, t in zip(arrived, to_two)
        ]
        return [(own[h] + (arrived[h] + direct[h])).astype(jnp.bfloat16) for h in range(2)]

    window_a = forward(own_pair_of(0))
    own_b = list(lax.optimization_barrier((own_pair_of(1), window_a[0]))[0])
    window_b = forward(own_b)
    windows = [window_a, window_b]

    query_parts = []
    results = []
    for chunk in range(CHUNKS):
        query_part, far, own = attention_back(
            queries, arriving, [w[0] for w in windows[chunk]], [w[1] for w in windows[chunk]],
            mask, chunk * chunk_groups, 0, chunk_groups,
        )
        query_parts.append(query_part)
        results.append((far, own))
    query_back = jnp.concatenate(query_parts, axis=1)

    totals = [backward(far, own) for far, own in results]
    return (
        query_back[None],
        jnp.concatenate([total[0] for total in totals], axis=1)[None],
        jnp.concatenate([total[1] for total in totals], axis=1)[None],
    )


def solution(mesh):
    return jax.shard_map(
        local_body,
        mesh=mesh,
        in_specs=(
            P("section", "ctx", None),
            P("section", "ctx", None),
            P("section", "ctx", None),
            P("section", "ctx", None),
            P(),
        ),
        out_specs=(P("section", "ctx", None), P("section", "ctx", None), P("section", "ctx", None)),
        check_vma=False,
    )
```

```python
import jax
import jax.numpy as jnp
from jax import lax
from jax.experimental import pallas as pl
from jax.experimental.pallas import tpu as pltpu
from jax.sharding import PartitionSpec as P


WINDOW = 1024
KV_HEADS = 8
CHUNKS = 2
GROUP = 2


SCORE_SCALE = 168.0 ** (-0.5)


def product(a, b, dims):
    return lax.dot_general(a, b, dims, preferred_element_type=jnp.float32)


def attention_back_kernel(at_ref, q_ref, do_ref, *refs):
    blocks = len(refs) - 4
    piece_refs = refs[:blocks]
    mask_ref = refs[blocks]
    dq_ref, far_ref, own_ref = refs[-3:]
    head_size = piece_refs[0].shape[2]
    heads = q_ref.shape[1] // head_size
    rows = q_ref.shape[0]
    allowed = mask_ref[...] > 0
    keys = jnp.concatenate([ref[0] for ref in piece_refs], axis=0)
    values = jnp.concatenate([ref[1] for ref in piece_refs], axis=0)
    queries = jnp.concatenate([q_ref[:, h * head_size:(h + 1) * head_size] for h in range(heads)], axis=0)
    grads = jnp.concatenate([do_ref[:, h * head_size:(h + 1) * head_size] for h in range(heads)], axis=0)
    allowed = jnp.concatenate([allowed] * heads, axis=0)
    nt = (((1,), (1,)), ((), ()))
    nn = (((1,), (0,)), ((), ()))
    scores = SCORE_SCALE * product(queries, keys, nt)
    scores = jnp.where(allowed, scores, -jnp.inf)
    highest = jnp.max(scores, axis=-1, keepdims=True)
    shifted_exp = jnp.exp(scores - highest)
    weights = shifted_exp * (1.0 / jnp.sum(shifted_exp, axis=-1, keepdims=True))
    weight_half = weights.astype(jnp.bfloat16)
    attended = product(weight_half, values, nn).astype(jnp.bfloat16)
    row_dot = jnp.sum(attended.astype(jnp.float32) * grads.astype(jnp.float32), axis=-1, keepdims=True)
    weight_grad = product(grads, values, nt)
    score_grad = (weights * (weight_grad - row_dot)).astype(jnp.bfloat16)
    query_back = SCORE_SCALE * product(score_grad, keys, nn)
    for h in range(heads):
        dq_ref[:, h * head_size:(h + 1) * head_size] = query_back[h * rows:(h + 1) * rows].astype(dq_ref.dtype)
    key_back = (SCORE_SCALE * product(queries.T, score_grad, nn)).T
    value_back = product(grads.T, weight_half, nn).T
    for block in range(blocks - 1):
        lines = slice(block * rows, (block + 1) * rows)
        far_ref[block, 0] = key_back[lines].astype(far_ref.dtype)
        far_ref[block, 1] = value_back[lines].astype(far_ref.dtype)
    own_ref[0] = key_back[(blocks - 1) * rows:]
    own_ref[1] = value_back[(blocks - 1) * rows:]


def attention_back(queries, grads, window_pieces, allowed, query_group, kv_group, groups):
    rows, width = queries.shape
    head_size = width // (GROUP * KV_HEADS)
    group_width = GROUP * head_size
    span = rows * len(window_pieces)
    q_spec = pl.BlockSpec((rows, group_width), lambda g, at: (0, g + at[0]))
    piece_spec = pl.BlockSpec((2, rows, head_size), lambda g, at: (0, 0, g + at[1]))
    mask_spec = pl.BlockSpec((rows, span), lambda g, at: (0, 0))
    far_spec = pl.BlockSpec((len(window_pieces) - 1, 2, rows, head_size), lambda g, at: (0, 0, 0, g))
    own_spec = pl.BlockSpec((2, rows, head_size), lambda g, at: (0, 0, g))
    inputs = [queries, grads, *window_pieces, allowed]
    dq_spec = pl.BlockSpec((rows, group_width), lambda g, at: (0, g))
    grid_spec = pltpu.PrefetchScalarGridSpec(
        num_scalar_prefetch=1,
        grid=(groups,),
        in_specs=[q_spec, q_spec] + [piece_spec] * len(window_pieces) + [mask_spec],
        out_specs=[dq_spec, far_spec, own_spec],
    )
    chunk_width = groups * head_size
    return pl.pallas_call(
        attention_back_kernel,
        grid_spec=grid_spec,
        out_shape=[
            jax.ShapeDtypeStruct((rows, groups * group_width), jnp.bfloat16),
            jax.ShapeDtypeStruct((len(window_pieces) - 1, 2, rows, chunk_width), jnp.bfloat16),
            jax.ShapeDtypeStruct((2, rows, chunk_width), jnp.float32),
        ],
        compiler_params=pltpu.CompilerParams(vmem_limit_bytes=60 * 1024 * 1024),
    )(jnp.array([query_group, kv_group], jnp.int32), *inputs)


def passed_along(shard, axis, by):
    count = lax.axis_size(axis)
    return lax.ppermute(shard, axis, [(i, (i + by) % count) for i in range(count)])


def shifted(value, axis, steps):
    count = lax.axis_size(axis)
    initial, last = (max(0, -steps), min(count, count - steps))
    return lax.ppermute(value, axis, [(source, source + steps) for source in range(initial, last)])


def doc_number(positions, doc_lengths):
    ends = jnp.cumsum(doc_lengths)
    return jnp.sum((positions[:, None] >= ends[None, :]).astype(jnp.int32), axis=1)


def window_mask(query_pos, key_pos, doc_lengths):
    same_doc = (
        doc_number(query_pos, doc_lengths)[:, None] == doc_number(key_pos, doc_lengths)[None, :]
    )
    spacing = query_pos[:, None] - key_pos[None, :]
    return same_doc & (spacing >= 0) & (spacing < WINDOW) & (key_pos[None, :] >= 0)


def local_body(query_rows, key_rows, value_rows, finished_grad, doc_lengths):
    queries = query_rows[0]
    keys_here = key_rows[0]
    values_here = value_rows[0]
    count_rows = queries.shape[0]
    pair_width = keys_here.shape[1]
    head_size = pair_width // KV_HEADS
    rank_here = lax.axis_index("ctx")
    first_pos = rank_here * count_rows
    arriving = passed_along(finished_grad, "section", -1)[0]
    query_pos = first_pos + jnp.arange(count_rows, dtype=jnp.int32)
    key_pos = first_pos - WINDOW + jnp.arange(WINDOW + count_rows, dtype=jnp.int32)
    allowed = window_mask(query_pos, key_pos, doc_lengths).astype(jnp.float32)
    chunk_groups = KV_HEADS // CHUNKS
    chunk_width = chunk_groups * head_size
    mask = allowed.astype(jnp.bfloat16)

    def own_pair_of(chunk):
        cols = slice(chunk * chunk_width, (chunk + 1) * chunk_width)
        return jnp.stack([keys_here[:, cols], values_here[:, cols]])

    odd = (rank_here % 2) == 1

    def partner(value):
        count = lax.axis_size("ctx")
        return lax.ppermute(value, "ctx", [(i, i ^ 1) for i in range(count)])

    def forward(own):
        minus_two = shifted(own, "ctx", 2)
        minus_one = partner(jnp.where(odd, minus_two, own))
        minus_four = shifted(minus_two, "ctx", 2)
        minus_three = partner(jnp.where(odd, minus_four, minus_two))
        return [minus_four, minus_three, minus_two, minus_one, own]

    def backward(far, own):
        passed = partner(jnp.stack([far[3], far[1]])).astype(jnp.float32)
        zero = jnp.zeros_like(passed[0])
        to_four = far[0].astype(jnp.float32) + jnp.where(odd, passed[1], zero)
        to_two = far[2].astype(jnp.float32) + jnp.where(odd, passed[0], passed[1])
        direct = jnp.where(odd, zero, passed[0])
        arrived = shifted(to_four.astype(jnp.bfloat16), "ctx", -2).astype(jnp.float32)
        arrived = shifted((arrived + to_two).astype(jnp.bfloat16), "ctx", -2).astype(jnp.float32)
        return (own + (arrived + direct)).astype(jnp.bfloat16)

    window_a = forward(own_pair_of(0))
    own_b = lax.optimization_barrier((own_pair_of(1), window_a[0]))[0]
    window_b = forward(own_b)
    windows = [window_a, window_b]

    query_parts = []
    results = []
    for chunk in range(CHUNKS):
        query_part, far, own = attention_back(
            queries, arriving, windows[chunk], mask, chunk * chunk_groups, 0, chunk_groups
        )
        query_parts.append(query_part)
        results.append((far, own))
    query_back = jnp.concatenate(query_parts, axis=1)

    totals = [backward(far, own) for far, own in results]
    return (
        query_back[None],
        jnp.concatenate([total[0] for total in totals], axis=1)[None],
        jnp.concatenate([total[1] for total in totals], axis=1)[None],
    )


def solution(mesh):
    return jax.shard_map(
        local_body,
        mesh=mesh,
        in_specs=(
            P("section", "ctx", None),
            P("section", "ctx", None),
            P("section", "ctx", None),
            P("section", "ctx", None),
            P(),
        ),
        out_specs=(P("section", "ctx", None), P("section", "ctx", None), P("section", "ctx", None)),
        check_vma=False,
    )
```
